32 devices in a mesh: group: 2 (over y), inp: 4 (over z), tm: 2 (over x), pol: 2 (over core).
Axes of the slice: x: 2, y: 2, z: 4, core: 2. Of those that a mesh axis runs over, the one named last changes fastest.
Arguments:
- voltages: bfloat16 [1024, 65536], P(('group', 'inp'), ('tm', 'pol')), parts along dimension 0, may hold values from -6 to 6
Outputs:
- visibilities: float32 [1024, 2, 512, 512], P(('group', 'inp', 'tm'), None, 'pol'), parts along dimension 0
The draws below stay inside these ranges and needn't reach their ends.
There are 2 independent parts, one for each index of `group`. The reference program is written for one: setup_inputs(seed, part) draws one part's arguments, and reference() takes and returns one part's arrays. A program takes and returns all parts, laid end to end along the dimension named above; each array names one. Nothing has to cross between parts.
All inputs are finite; a program needn't handle non-finite values.
Results may differ from the reference program's by a relative error of at most 0.0054.
Values may be sent and summed in bfloat16 or wider, within the bound.
No kernel may reach another device: no remote copies, remote signals or barrier semaphores. Data moves between devices by JAX's collectives and lax.ppermute only.
A program may use at most 256 MiB of HBM per device.

```python
import math
import jax
import jax.numpy as jnp
from jax import lax

INPUTS = 512
CH = 512
TAPS = 16
SPECTRA = 64
SAMPLES = 65536


def levels(key, dims, cuts, low, high):
    factor_of, own = 1.0, jax.random.fold_in(key, 6)
    for axis_at, shards_of in cuts:
        steps = jnp.exp(jax.random.uniform(jax.random.fold_in(own, axis_at), (shards_of,), jnp.float32, low / len(cuts), high / len(cuts)))
        factor_of = factor_of * jnp.repeat(steps, dims[axis_at] // shards_of).reshape([-1 if axis == axis_at else 1 for axis in range(len(dims))])
    return factor_of


def scatter_about(stream_key, dims, spread, bound, pieces=(), kind=jnp.bfloat16):
    array = spread * jax.random.normal(stream_key, dims, jnp.float32)
    if pieces:
        array = array * levels(stream_key, dims, pieces, -0.22, 0.18)
    return jnp.clip(array, -bound, bound).astype(kind)


def setup_inputs(seed: int = 0, part: int = 0) -> dict:
    seeds = jax.random.split(jax.random.key(seed), 2)
    part_splits = jax.random.split(jax.random.fold_in(seeds[1], part), 2)
    voltages = scatter_about(part_splits[0], (INPUTS, SAMPLES), 1.0, 6.0, ((0, 4), (1, 4)))
    return dict(voltages=voltages)


def prototype(tap_count, frame_len):
    length = tap_count * frame_len
    sample = lax.broadcasted_iota(jnp.int32, (length,), 0).astype(jnp.float32)
    centred = (sample - (length - 1) / 2.0) / frame_len
    window = 0.5 - 0.5 * jnp.cos(2.0 * math.pi * (sample + 0.5) / length)
    angle = math.pi * centred
    filter_taps = jnp.sin(angle) / angle * window
    filter_taps = filter_taps / jnp.sqrt(jnp.sum(filter_taps * filter_taps))
    return filter_taps.reshape(tap_count, frame_len).astype(jnp.float32)

def dft_table(frame_len):
    sample_idx = lax.broadcasted_iota(jnp.int32, (frame_len, frame_len // 2), 0)
    channel_idx = lax.broadcasted_iota(jnp.int32, (frame_len, frame_len // 2), 1)
    phase = (sample_idx * channel_idx % frame_len).astype(jnp.float32) * (2.0 * math.pi / frame_len)
    table = jnp.stack([jnp.cos(phase), -jnp.sin(phase)], axis=2)
    return table.reshape(frame_len, frame_len).astype(jnp.bfloat16)

def reference(voltages):
    frame_len = 2 * CH
    frames = voltages.reshape(INPUTS, SPECTRA, frame_len)
    extended = jnp.concatenate([jnp.zeros((INPUTS, TAPS - 1, frame_len), voltages.dtype), frames], axis=1)
    filter_taps = prototype(TAPS, frame_len)
    filtered = jnp.zeros((INPUTS, SPECTRA, frame_len), jnp.float32)
    for tap_index in range(TAPS):
        filtered = filtered + filter_taps[tap_index] * extended[:, tap_index:tap_index + SPECTRA, :].astype(jnp.float32)
    filtered = filtered.astype(jnp.bfloat16)
    spectra = lax.dot_general(dft_table(frame_len), filtered.reshape(INPUTS * SPECTRA, frame_len), (((0,), (1,)), ((), ())), preferred_element_type=jnp.float32)
    spectra = spectra.astype(jnp.bfloat16).reshape(CH, 2, INPUTS, SPECTRA)

    def one_channel(channel_block):
        left_rows = jnp.concatenate([channel_block[0], channel_block[1]], axis=-1)
        right_imag = jnp.concatenate([-channel_block[1], channel_block[0]], axis=-1)
        real_part = jnp.dot(left_rows, left_rows.T, preferred_element_type=jnp.float32)
        imag_part = jnp.dot(left_rows, right_imag.T, preferred_element_type=jnp.float32)
        return jnp.stack([real_part, imag_part]) * (1.0 / SPECTRA)
    return lax.map(one_channel, spectra)
```

```python
import math

import jax
import jax.numpy as jnp
from jax import lax
from jax.sharding import PartitionSpec as P

CH = 512
TAPS = 16


def shifted(block, axis, distance):
    devices = range(lax.axis_size(axis))
    route = [(i - distance, i) for i in devices if i - distance in devices]
    return lax.ppermute(block, axis, route)


def prototype(tap_count, frame_len):
    length = tap_count * frame_len
    sample = lax.broadcasted_iota(jnp.int32, (length,), 0).astype(jnp.float32)
    centred = (sample - (length - 1) / 2.0) / frame_len
    window = 0.5 - 0.5 * jnp.cos(2.0 * math.pi * (sample + 0.5) / length)
    angle = math.pi * centred
    filter_taps = jnp.sin(angle) / angle * window
    filter_taps = filter_taps / jnp.sqrt(jnp.sum(filter_taps * filter_taps))
    return filter_taps.reshape(tap_count, frame_len)


def dft_table_t(frame_len):
    channel_idx = lax.broadcasted_iota(jnp.int32, (frame_len // 2, frame_len), 0)
    sample_idx = lax.broadcasted_iota(jnp.int32, (frame_len // 2, frame_len), 1)
    phase = (sample_idx * channel_idx % frame_len).astype(jnp.float32) * (2.0 * math.pi / frame_len)
    table = jnp.stack([jnp.cos(phase), -jnp.sin(phase)], axis=1)
    return table.reshape(frame_len, frame_len).astype(jnp.bfloat16)


def per_device(voltages):
    inputs_here = voltages.shape[0]
    frame_len = 2 * CH
    spectra_here = voltages.shape[1] // frame_len
    frames = voltages.reshape(inputs_here, spectra_here, frame_len).transpose(1, 0, 2)
    last_frames = frames[spectra_here - (TAPS - 1) :]
    history = shifted(last_frames, ("tm", "pol"), 1)
    extended = jnp.concatenate([history, frames], axis=0)
    filter_taps = prototype(TAPS, frame_len)
    filtered = jnp.zeros((spectra_here, inputs_here, frame_len), jnp.float32)
    for tap_index in range(TAPS):
        filtered = filtered + filter_taps[tap_index] * extended[
            tap_index : tap_index + spectra_here
        ].astype(jnp.float32)
    filtered = filtered.astype(jnp.bfloat16)
    spectra = lax.dot_general(
        dft_table_t(frame_len),
        filtered.reshape(spectra_here * inputs_here, frame_len),
        (((1,), (1,)), ((), ())),
        preferred_element_type=jnp.float32,
    )
    spectra = spectra.astype(jnp.bfloat16).reshape(CH, 2, spectra_here, inputs_here)
    inp_size = lax.axis_size("inp")
    tm_size = lax.axis_size("tm")
    pol_size = lax.axis_size("pol")
    own_channels = CH // (inp_size * tm_size)
    received = lax.all_to_all(spectra, ("inp", "tm"), split_axis=0, concat_axis=0, tiled=True)
    received = received.reshape(inp_size, tm_size, own_channels, 2, spectra_here, inputs_here)
    gathered = lax.all_gather(received, "pol", axis=0, tiled=False)
    blocks = gathered.transpose(3, 2, 0, 4, 5, 1, 6)
    depth = tm_size * pol_size * 2 * spectra_here
    cols = inp_size * inputs_here
    left_all = blocks.reshape(own_channels, depth, cols)
    right_imag = jnp.stack([-blocks[:, :, :, 1], blocks[:, :, :, 0]], axis=3).reshape(
        own_channels, depth, cols
    )
    right = jnp.stack([left_all, right_imag], axis=1)
    rows_here = cols // pol_size
    row_start = lax.axis_index("pol") * rows_here
    own_rows = lax.dynamic_slice_in_dim(left_all, row_start, rows_here, 2)
    own_rows = jnp.broadcast_to(own_rows[:, None], (own_channels, 2, depth, rows_here))
    summed = lax.dot_general(
        own_rows,
        right,
        (((2,), (2,)), ((0, 1), (0, 1))),
        preferred_element_type=jnp.float32,
    )
    return summed * (1.0 / (depth // 2))


def solution(mesh):
    return jax.shard_map(
        per_device,
        mesh=mesh,
        in_specs=(P(("group", "inp"), ("tm", "pol")),),
        out_specs=P(("group", "inp", "tm"), None, "pol", None),
        check_vma=False,
    )
```

```python
import math

import jax
import jax.numpy as jnp
from jax import lax
from jax.sharding import PartitionSpec as P

CH = 512
TAPS = 16


def shifted(block, axis, distance):
    devices = range(lax.axis_size(axis))
    route = [(i - distance, i) for i in devices if i - distance in devices]
    return lax.ppermute(block, axis, route)


def prototype(tap_count, frame_len):
    length = tap_count * frame_len
    sample = lax.broadcasted_iota(jnp.int32, (length,), 0).astype(jnp.float32)
    centred = (sample - (length - 1) / 2.0) / frame_len
    window = 0.5 - 0.5 * jnp.cos(2.0 * math.pi * (sample + 0.5) / length)
    angle = math.pi * centred
    filter_taps = jnp.sin(angle) / angle * window
    filter_taps = filter_taps / jnp.sqrt(jnp.sum(filter_taps * filter_taps))
    return filter_taps.reshape(tap_count, frame_len)


def dft_table_t(frame_len):
    channel_idx = lax.broadcasted_iota(jnp.int32, (frame_len // 2, frame_len), 0)
    sample_idx = lax.broadcasted_iota(jnp.int32, (frame_len // 2, frame_len), 1)
    phase = (sample_idx * channel_idx % frame_len).astype(jnp.float32) * (2.0 * math.pi / frame_len)
    table = jnp.stack([jnp.cos(phase), -jnp.sin(phase)], axis=1)
    return table.reshape(frame_len, frame_len).astype(jnp.bfloat16)


def per_device(voltages):
    inputs_here = voltages.shape[0]
    frame_len = 2 * CH
    spectra_here = voltages.shape[1] // frame_len
    frames = voltages.reshape(inputs_here, spectra_here, frame_len).transpose(1, 0, 2)
    last_frames = frames[spectra_here - (TAPS - 1) :]
    history = shifted(last_frames, ("tm", "pol"), 1)
    extended = jnp.concatenate([history, frames], axis=0)
    filter_taps = prototype(TAPS, frame_len)
    filtered = jnp.zeros((spectra_here, inputs_here, frame_len), jnp.float32)
    for tap_index in range(TAPS):
        filtered = filtered + filter_taps[tap_index] * extended[
            tap_index : tap_index + spectra_here
        ].astype(jnp.float32)
    filtered = filtered.astype(jnp.bfloat16)
    spectra = lax.dot_general(
        dft_table_t(frame_len),
        filtered.reshape(spectra_here * inputs_here, frame_len),
        (((1,), (1,)), ((), ())),
        preferred_element_type=jnp.float32,
    )
    spectra = spectra.astype(jnp.bfloat16).reshape(CH, 2, spectra_here, inputs_here)
    inp_size = lax.axis_size("inp")
    tm_size = lax.axis_size("tm")
    pol_size = lax.axis_size("pol")
    group_size = inp_size * tm_size
    own_channels = CH // group_size
    blocks = spectra.reshape(group_size, own_channels, 2, spectra_here, inputs_here)
    inp_at = lax.axis_index("inp")
    tm_at = lax.axis_index("tm")
    cols = inp_size * inputs_here
    half = jnp.zeros((own_channels, 2, tm_size, spectra_here, cols), jnp.bfloat16)
    for inp_step in range(inp_size):
        for tm_step in range(tm_size):
            target = ((inp_at + inp_step) % inp_size) * tm_size + (tm_at + tm_step) % tm_size
            block = lax.dynamic_index_in_dim(blocks, target, 0, keepdims=False)
            if inp_step or tm_step:
                route = [
                    (g, ((g // tm_size + inp_step) % inp_size) * tm_size + (g % tm_size + tm_step) % tm_size)
                    for g in range(group_size)
                ]
                block = lax.ppermute(block, ("inp", "tm"), route)
            source_inp = (inp_at + inp_size - inp_step) % inp_size
            half = lax.dynamic_update_slice(
                half, block[:, :, None], (0, 0, tm_step, 0, source_inp * inputs_here)
            )
    if pol_size == 2:
        partner = lax.ppermute(half, "pol", [(0, 1), (1, 0)])
        both = jnp.stack([half, partner], axis=1)
    else:
        both = lax.all_gather(half, "pol", axis=1, tiled=False)
    depth = pol_size * 2 * tm_size * spectra_here
    left_all = both.reshape(own_channels, depth, cols)
    rows_here = cols // pol_size
    row_start = lax.axis_index("pol") * rows_here
    own_rows = lax.dynamic_slice_in_dim(both, row_start, rows_here, 5)
    swapped = jnp.stack([own_rows[:, :, 1], -own_rows[:, :, 0]], axis=2)
    lhs = jnp.stack([own_rows, swapped], axis=1).reshape(own_channels, 2, depth, rows_here)
    summed = lax.dot_general(
        lhs,
        left_all,
        (((2,), (1,)), ((0,), (0,))),
        preferred_element_type=jnp.float32,
    )
    return summed * (1.0 / (depth // 2))


def solution(mesh):
    return jax.shard_map(
        per_device,
        mesh=mesh,
        in_specs=(P(("group", "inp"), ("tm", "pol")),),
        out_specs=P(("group", "inp", "tm"), None, "pol", None),
        check_vma=False,
    )
```

```python
import functools
import math

import jax
import jax.numpy as jnp
from jax import lax
from jax.experimental import pallas as pl
from jax.sharding import PartitionSpec as P

CH = 512
TAPS = 16


def shifted(block, axis, distance):
    devices = range(lax.axis_size(axis))
    route = [(i - distance, i) for i in devices if i - distance in devices]
    return lax.ppermute(block, axis, route)


def prototype(tap_count, frame_len):
    length = tap_count * frame_len
    sample = lax.broadcasted_iota(jnp.int32, (length,), 0).astype(jnp.float32)
    centred = (sample - (length - 1) / 2.0) / frame_len
    window = 0.5 - 0.5 * jnp.cos(2.0 * math.pi * (sample + 0.5) / length)
    angle = math.pi * centred
    filter_taps = jnp.sin(angle) / angle * window
    filter_taps = filter_taps / jnp.sqrt(jnp.sum(filter_taps * filter_taps))
    return filter_taps.reshape(tap_count, frame_len)


def dft_table_t(frame_len):
    channel_idx = lax.broadcasted_iota(jnp.int32, (frame_len // 2, frame_len), 0)
    sample_idx = lax.broadcasted_iota(jnp.int32, (frame_len // 2, frame_len), 1)
    phase = (sample_idx * channel_idx % frame_len).astype(jnp.float32) * (2.0 * math.pi / frame_len)
    table = jnp.stack([jnp.cos(phase), -jnp.sin(phase)], axis=1)
    return table.reshape(frame_len, frame_len).astype(jnp.bfloat16)


def per_device(voltages):
    inputs_here = voltages.shape[0]
    frame_len = 2 * CH
    spectra_here = voltages.shape[1] // frame_len
    frames = voltages.reshape(inputs_here, spectra_here, frame_len).transpose(1, 0, 2)
    last_frames = frames[spectra_here - (TAPS - 1) :]
    history = shifted(last_frames, ("tm", "pol"), 1)
    extended = jnp.concatenate([history, frames], axis=0)
    filter_taps = prototype(TAPS, frame_len)
    filtered = jnp.zeros((spectra_here, inputs_here, frame_len), jnp.float32)
    for tap_index in range(TAPS):
        filtered = filtered + filter_taps[tap_index] * extended[
            tap_index : tap_index + spectra_here
        ].astype(jnp.float32)
    filtered = filtered.astype(jnp.bfloat16)
    spectra = lax.dot_general(
        dft_table_t(frame_len),
        filtered.reshape(spectra_here * inputs_here, frame_len),
        (((1,), (1,)), ((), ())),
        preferred_element_type=jnp.float32,
    )
    spectra = spectra.astype(jnp.bfloat16).reshape(CH, 2, spectra_here, inputs_here)
    inp_size = lax.axis_size("inp")
    tm_size = lax.axis_size("tm")
    pol_size = lax.axis_size("pol")
    group_size = inp_size * tm_size
    own_channels = CH // group_size
    blocks = spectra.reshape(group_size, own_channels, 2, spectra_here, inputs_here)
    inp_at = lax.axis_index("inp")
    tm_at = lax.axis_index("tm")
    cols = inp_size * inputs_here
    chunks = 2 if own_channels % 2 == 0 else 1
    per_chunk = own_channels // chunks
    parts = [blocks[:, chunk * per_chunk : (chunk + 1) * per_chunk] for chunk in range(chunks)]
    out = None
    half = None
    for chunk in range(chunks):
        if chunk:
            half, parts[chunk] = lax.optimization_barrier((half, parts[chunk]))
        pieces = send_chunk(parts[chunk], inp_at, tm_at, inp_size, tm_size)
        if chunk:
            lhs, rhs = finish_chunk(half, pol_size, cols)
            out = correlate(lhs, rhs, out, (chunk - 1) * per_chunk, own_channels)
            out, pieces = lax.optimization_barrier((out, pieces))
        half = assemble_chunk(pieces, inp_at, inp_size, tm_size, cols)
    lhs, rhs = finish_chunk(half, pol_size, cols)
    return correlate(lhs, rhs, out, (chunks - 1) * per_chunk, own_channels)


def correlate_kernel(scale, lhs_ref, rhs_ref, *rest):
    out_ref = rest[-1]
    rows = out_ref.shape[2]
    for k in range(lhs_ref.shape[0]):
        acc = jnp.dot(lhs_ref[k], rhs_ref[k], preferred_element_type=jnp.float32) * scale
        out_ref[k, 0] = acc[:rows]
        out_ref[k, 1] = acc[rows:]


def correlate(lhs, rhs, prev, first_channel, own_channels):
    count, two_rows, depth = lhs.shape
    cols = rhs.shape[2]
    rows = two_rows // 2
    step = 2 if count % 2 == 0 else 1
    offset = first_channel // step
    in_specs = [
        pl.BlockSpec((step, two_rows, depth), lambda c: (c, 0, 0)),
        pl.BlockSpec((step, depth, cols), lambda c: (c, 0, 0)),
    ]
    args = [lhs, rhs]
    aliases = {}
    if prev is not None:
        in_specs.append(pl.BlockSpec(memory_space=pl.ANY))
        args.append(prev)
        aliases = {2: 0}
    flops = 2 * count * two_rows * depth * cols
    out_bytes = count * two_rows * cols * 4
    return pl.pallas_call(
        functools.partial(correlate_kernel, 1.0 / (depth // 2)),
        grid=(count // step,),
        in_specs=in_specs,
        out_specs=pl.BlockSpec((step, 2, rows, cols), lambda c: (c + offset, 0, 0, 0)),
        out_shape=jax.ShapeDtypeStruct((own_channels, 2, rows, cols), jnp.float32),
        input_output_aliases=aliases,
        cost_estimate=pl.CostEstimate(
            flops=flops, bytes_accessed=out_bytes + lhs.size * 2 + rhs.size * 2, transcendentals=0
        ),
    )(*args)


def send_chunk(blocks, inp_at, tm_at, inp_size, tm_size):
    group_size = blocks.shape[0]
    pieces = []
    for inp_step in range(inp_size):
        for tm_step in range(tm_size):
            target = ((inp_at + inp_step) % inp_size) * tm_size + (tm_at + tm_step) % tm_size
            block = lax.dynamic_index_in_dim(blocks, target, 0, keepdims=False)
            if inp_step or tm_step:
                route = [
                    (g, ((g // tm_size + inp_step) % inp_size) * tm_size + (g % tm_size + tm_step) % tm_size)
                    for g in range(group_size)
                ]
                block = lax.ppermute(block, ("inp", "tm"), route)
            pieces.append(block)
    return pieces


def assemble_chunk(pieces, inp_at, inp_size, tm_size, cols):
    own_channels, _, spectra_here, inputs_here = pieces[0].shape
    half = jnp.zeros((own_channels, 2, tm_size, spectra_here, cols), jnp.bfloat16)
    for inp_step in range(inp_size):
        for tm_step in range(tm_size):
            block = pieces[inp_step * tm_size + tm_step]
            source_inp = (inp_at + inp_size - inp_step) % inp_size
            half = lax.dynamic_update_slice(
                half, block[:, :, None], (0, 0, tm_step, 0, source_inp * inputs_here)
            )
    return half


def finish_chunk(half, pol_size, cols):
    own_channels, _, tm_size, spectra_here, _ = half.shape
    if pol_size == 2:
        partner = lax.ppermute(half, "pol", [(0, 1), (1, 0)])
        both = jnp.stack([half, partner], axis=1)
    else:
        both = lax.all_gather(half, "pol", axis=1, tiled=False)
    depth = pol_size * 2 * tm_size * spectra_here
    left_all = both.reshape(own_channels, depth, cols)
    rows_here = cols // pol_size
    row_start = lax.axis_index("pol") * rows_here
    own_rows = lax.dynamic_slice_in_dim(both, row_start, rows_here, 5)
    swapped = jnp.stack([own_rows[:, :, 1], -own_rows[:, :, 0]], axis=2)
    lhs = jnp.stack([own_rows, swapped], axis=1).reshape(own_channels, 2, depth, rows_here)
    lhs = lhs.transpose(0, 1, 3, 2).reshape(own_channels, 2 * rows_here, depth)
    return lhs, left_all


def solution(mesh):
    return jax.shard_map(
        per_device,
        mesh=mesh,
        in_specs=(P(("group", "inp"), ("tm", "pol")),),
        out_specs=P(("group", "inp", "tm"), None, "pol", None),
        check_vma=False,
    )
```

```python
import functools
import math

import jax
import jax.numpy as jnp
from jax import lax
from jax.experimental import pallas as pl
from jax.sharding import PartitionSpec as P

CH = 512
TAPS = 16


def shifted(block, axis, distance):
    devices = range(lax.axis_size(axis))
    route = [(i - distance, i) for i in devices if i - distance in devices]
    return lax.ppermute(block, axis, route)


def prototype(tap_count, frame_len):
    length = tap_count * frame_len
    sample = lax.broadcasted_iota(jnp.int32, (length,), 0).astype(jnp.float32)
    centred = (sample - (length - 1) / 2.0) / frame_len
    window = 0.5 - 0.5 * jnp.cos(2.0 * math.pi * (sample + 0.5) / length)
    angle = math.pi * centred
    filter_taps = jnp.sin(angle) / angle * window
    filter_taps = filter_taps / jnp.sqrt(jnp.sum(filter_taps * filter_taps))
    return filter_taps.reshape(tap_count, frame_len)


def dft_table_t(frame_len):
    channel_idx = lax.broadcasted_iota(jnp.int32, (frame_len // 2, frame_len), 0)
    sample_idx = lax.broadcasted_iota(jnp.int32, (frame_len // 2, frame_len), 1)
    phase = (sample_idx * channel_idx % frame_len).astype(jnp.float32) * (2.0 * math.pi / frame_len)
    table = jnp.stack([jnp.cos(phase), -jnp.sin(phase)], axis=1)
    return table.reshape(frame_len, frame_len).astype(jnp.bfloat16)


def per_device(voltages):
    inputs_here = voltages.shape[0]
    frame_len = 2 * CH
    spectra_here = voltages.shape[1] // frame_len
    frames = voltages.reshape(inputs_here, spectra_here, frame_len).transpose(1, 0, 2)
    last_frames = frames[spectra_here - (TAPS - 1) :]
    history = shifted(last_frames, ("tm", "pol"), 1)
    extended = jnp.concatenate([history, frames], axis=0)
    filter_taps = prototype(TAPS, frame_len)
    filtered = jnp.zeros((spectra_here, inputs_here, frame_len), jnp.float32)
    for tap_index in range(TAPS):
        filtered = filtered + filter_taps[tap_index] * extended[
            tap_index : tap_index + spectra_here
        ].astype(jnp.float32)
    filtered = filtered.astype(jnp.bfloat16)
    spectra = lax.dot_general(
        dft_table_t(frame_len),
        filtered.reshape(spectra_here * inputs_here, frame_len),
        (((1,), (1,)), ((), ())),
        preferred_element_type=jnp.float32,
    )
    spectra = spectra.astype(jnp.bfloat16).reshape(CH, 2, spectra_here, inputs_here)
    inp_size = lax.axis_size("inp")
    tm_size = lax.axis_size("tm")
    pol_size = lax.axis_size("pol")
    group_size = inp_size * tm_size
    own_channels = CH // group_size
    blocks = spectra.reshape(group_size, own_channels, 2, spectra_here, inputs_here)
    inp_at = lax.axis_index("inp")
    tm_at = lax.axis_index("tm")
    cols = inp_size * inputs_here
    chunks = 4 if own_channels % 8 == 0 else 1
    per_chunk = own_channels // chunks
    parts = [blocks[:, chunk * per_chunk : (chunk + 1) * per_chunk] for chunk in range(chunks)]
    out = None
    half = None
    for chunk in range(chunks):
        if chunk:
            half, parts[chunk] = lax.optimization_barrier((half, parts[chunk]))
        pieces = send_chunk(parts[chunk], inp_at, tm_at, inp_size, tm_size)
        if chunk:
            lhs, rhs = finish_chunk(half, pol_size, cols)
            out = correlate(lhs, rhs, out, (chunk - 1) * per_chunk, own_channels)
            out, pieces = lax.optimization_barrier((out, pieces))
        half = assemble_chunk(pieces, inp_at, inp_size, tm_size, cols)
    lhs, rhs = finish_chunk(half, pol_size, cols)
    return correlate(lhs, rhs, out, (chunks - 1) * per_chunk, own_channels)


def correlate_kernel(scale, lhs_ref, rhs_ref, *rest):
    out_ref = rest[-1]
    rows = out_ref.shape[2]
    for k in range(lhs_ref.shape[0]):
        acc = jnp.dot(lhs_ref[k], rhs_ref[k], preferred_element_type=jnp.float32) * scale
        out_ref[k, 0] = acc[:rows]
        out_ref[k, 1] = acc[rows:]


def correlate(lhs, rhs, prev, first_channel, own_channels):
    count, two_rows, depth = lhs.shape
    cols = rhs.shape[2]
    rows = two_rows // 2
    step = 2 if count % 2 == 0 else 1
    offset = first_channel // step
    in_specs = [
        pl.BlockSpec((step, two_rows, depth), lambda c: (c, 0, 0)),
        pl.BlockSpec((step, depth, cols), lambda c: (c, 0, 0)),
    ]
    args = [lhs, rhs]
    aliases = {}
    if prev is not None:
        in_specs.append(pl.BlockSpec(memory_space=pl.ANY))
        args.append(prev)
        aliases = {2: 0}
    flops = 2 * count * two_rows * depth * cols
    out_bytes = count * two_rows * cols * 4
    return pl.pallas_call(
        functools.partial(correlate_kernel, 1.0 / (depth // 2)),
        grid=(count // step,),
        in_specs=in_specs,
        out_specs=pl.BlockSpec((step, 2, rows, cols), lambda c: (c + offset, 0, 0, 0)),
        out_shape=jax.ShapeDtypeStruct((own_channels, 2, rows, cols), jnp.float32),
        input_output_aliases=aliases,
        cost_estimate=pl.CostEstimate(
            flops=flops, bytes_accessed=out_bytes + lhs.size * 2 + rhs.size * 2, transcendentals=0
        ),
    )(*args)


def send_chunk(blocks, inp_at, tm_at, inp_size, tm_size):
    group_size = blocks.shape[0]
    pieces = []
    for inp_step in range(inp_size):
        for tm_step in range(tm_size):
            target = ((inp_at + inp_step) % inp_size) * tm_size + (tm_at + tm_step) % tm_size
            block = lax.dynamic_index_in_dim(blocks, target, 0, keepdims=False)
            if inp_step or tm_step:
                route = [
                    (g, ((g // tm_size + inp_step) % inp_size) * tm_size + (g % tm_size + tm_step) % tm_size)
                    for g in range(group_size)
                ]
                block = lax.ppermute(block, ("inp", "tm"), route)
            pieces.append(block)
    return pieces


def assemble_chunk(pieces, inp_at, inp_size, tm_size, cols):
    own_channels, _, spectra_here, inputs_here = pieces[0].shape
    half = jnp.zeros((own_channels, 2, tm_size, spectra_here, cols), jnp.bfloat16)
    for inp_step in range(inp_size):
        for tm_step in range(tm_size):
            block = pieces[inp_step * tm_size + tm_step]
            source_inp = (inp_at + inp_size - inp_step) % inp_size
            half = lax.dynamic_update_slice(
                half, block[:, :, None], (0, 0, tm_step, 0, source_inp * inputs_here)
            )
    return half


def finish_chunk(half, pol_size, cols):
    own_channels, _, tm_size, spectra_here, _ = half.shape
    if pol_size == 2:
        partner = lax.ppermute(half, "pol", [(0, 1), (1, 0)])
        both = jnp.stack([half, partner], axis=1)
    else:
        both = lax.all_gather(half, "pol", axis=1, tiled=False)
    depth = pol_size * 2 * tm_size * spectra_here
    left_all = both.reshape(own_channels, depth, cols)
    rows_here = cols // pol_size
    row_start = lax.axis_index("pol") * rows_here
    own_rows = lax.dynamic_slice_in_dim(both, row_start, rows_here, 5)
    swapped = jnp.stack([own_rows[:, :, 1], -own_rows[:, :, 0]], axis=2)
    lhs = jnp.stack([own_rows, swapped], axis=1).reshape(own_channels, 2, depth, rows_here)
    lhs = lhs.transpose(0, 1, 3, 2).reshape(own_channels, 2 * rows_here, depth)
    return lhs, left_all


def solution(mesh):
    return jax.shard_map(
        per_device,
        mesh=mesh,
        in_specs=(P(("group", "inp"), ("tm", "pol")),),
        out_specs=P(("group", "inp", "tm"), None, "pol", None),
        check_vma=False,
    )
```

```python
import functools
import math

import jax
import jax.numpy as jnp
from jax import lax
from jax.experimental import pallas as pl
from jax.sharding import PartitionSpec as P

CH = 512
TAPS = 16


def shifted(block, axis, distance):
    devices = range(lax.axis_size(axis))
    route = [(i - distance, i) for i in devices if i - distance in devices]
    return lax.ppermute(block, axis, route)


def prototype(tap_count, frame_len):
    length = tap_count * frame_len
    sample = lax.broadcasted_iota(jnp.int32, (length,), 0).astype(jnp.float32)
    centred = (sample - (length - 1) / 2.0) / frame_len
    window = 0.5 - 0.5 * jnp.cos(2.0 * math.pi * (sample + 0.5) / length)
    angle = math.pi * centred
    filter_taps = jnp.sin(angle) / angle * window
    filter_taps = filter_taps / jnp.sqrt(jnp.sum(filter_taps * filter_taps))
    return filter_taps.reshape(tap_count, frame_len)


def dft_table_t(frame_len):
    channel_idx = lax.broadcasted_iota(jnp.int32, (frame_len // 2, frame_len), 0)
    sample_idx = lax.broadcasted_iota(jnp.int32, (frame_len // 2, frame_len), 1)
    phase = (sample_idx * channel_idx % frame_len).astype(jnp.float32) * (2.0 * math.pi / frame_len)
    table = jnp.stack([jnp.cos(phase), -jnp.sin(phase)], axis=1)
    return table.reshape(frame_len, frame_len).astype(jnp.bfloat16)


def per_device(voltages):
    inputs_here = voltages.shape[0]
    frame_len = 2 * CH
    spectra_here = voltages.shape[1] // frame_len
    frames = voltages.reshape(inputs_here, spectra_here, frame_len).transpose(1, 0, 2)
    history = shifted(voltages[:, (spectra_here - (TAPS - 1)) * frame_len :], ("tm", "pol"), 1)
    history = history.reshape(inputs_here, TAPS - 1, frame_len)
    filter_taps = prototype(TAPS, frame_len)
    own_part = []
    for s in range(spectra_here):
        total = None
        for tap_index in range(max(0, TAPS - 1 - s), TAPS):
            term = filter_taps[tap_index] * frames[s + tap_index - (TAPS - 1)].astype(jnp.float32)
            total = term if total is None else total + term
        own_part.append(total)
    own_part = lax.optimization_barrier(jnp.stack(own_part))
    hist_part = []
    for s in range(spectra_here):
        total = jnp.zeros((inputs_here, frame_len), jnp.float32)
        for tap_index in range(0, max(0, TAPS - 1 - s)):
            total = total + filter_taps[tap_index] * history[:, s + tap_index].astype(jnp.float32)
        hist_part.append(total)
    filtered = (own_part + jnp.stack(hist_part)).astype(jnp.bfloat16)
    spectra = lax.dot_general(
        dft_table_t(frame_len),
        filtered.reshape(spectra_here * inputs_here, frame_len),
        (((1,), (1,)), ((), ())),
        preferred_element_type=jnp.float32,
    )
    spectra = spectra.astype(jnp.bfloat16).reshape(CH, 2, spectra_here, inputs_here)
    inp_size = lax.axis_size("inp")
    tm_size = lax.axis_size("tm")
    pol_size = lax.axis_size("pol")
    group_size = inp_size * tm_size
    own_channels = CH // group_size
    blocks = spectra.reshape(group_size, own_channels, 2, spectra_here, inputs_here)
    inp_at = lax.axis_index("inp")
    tm_at = lax.axis_index("tm")
    cols = inp_size * inputs_here
    chunks = 4 if own_channels % 8 == 0 else 1
    per_chunk = own_channels // chunks
    parts = [blocks[:, chunk * per_chunk : (chunk + 1) * per_chunk] for chunk in range(chunks)]
    out = None
    half = None
    for chunk in range(chunks):
        if chunk:
            half, parts[chunk] = lax.optimization_barrier((half, parts[chunk]))
        pieces = send_chunk(parts[chunk], inp_at, tm_at, inp_size, tm_size)
        if chunk:
            lhs, rhs = finish_chunk(half, pol_size, cols)
            out = correlate(lhs, rhs, out, (chunk - 1) * per_chunk, own_channels)
            out, pieces = lax.optimization_barrier((out, pieces))
        half = assemble_chunk(pieces, inp_at, inp_size, tm_size, cols)
    lhs, rhs = finish_chunk(half, pol_size, cols)
    return correlate(lhs, rhs, out, (chunks - 1) * per_chunk, own_channels)


def correlate_kernel(scale, lhs_ref, rhs_ref, *rest):
    out_ref = rest[-1]
    rows = out_ref.shape[2]
    for k in range(lhs_ref.shape[0]):
        acc = jnp.dot(lhs_ref[k], rhs_ref[k], preferred_element_type=jnp.float32) * scale
        out_ref[k, 0] = acc[:rows]
        out_ref[k, 1] = acc[rows:]


def correlate(lhs, rhs, prev, first_channel, own_channels):
    count, two_rows, depth = lhs.shape
    cols = rhs.shape[2]
    rows = two_rows // 2
    step = 2 if count % 2 == 0 else 1
    offset = first_channel // step
    in_specs = [
        pl.BlockSpec((step, two_rows, depth), lambda c: (c, 0, 0)),
        pl.BlockSpec((step, depth, cols), lambda c: (c, 0, 0)),
    ]
    args = [lhs, rhs]
    aliases = {}
    if prev is not None:
        in_specs.append(pl.BlockSpec(memory_space=pl.ANY))
        args.append(prev)
        aliases = {2: 0}
    flops = 2 * count * two_rows * depth * cols
    out_bytes = count * two_rows * cols * 4
    return pl.pallas_call(
        functools.partial(correlate_kernel, 1.0 / (depth // 2)),
        grid=(count // step,),
        in_specs=in_specs,
        out_specs=pl.BlockSpec((step, 2, rows, cols), lambda c: (c + offset, 0, 0, 0)),
        out_shape=jax.ShapeDtypeStruct((own_channels, 2, rows, cols), jnp.float32),
        input_output_aliases=aliases,
        cost_estimate=pl.CostEstimate(
            flops=flops, bytes_accessed=out_bytes + lhs.size * 2 + rhs.size * 2, transcendentals=0
        ),
    )(*args)


def send_chunk(blocks, inp_at, tm_at, inp_size, tm_size):
    group_size = blocks.shape[0]
    pieces = []
    for inp_step in range(inp_size):
        for tm_step in range(tm_size):
            target = ((inp_at + inp_step) % inp_size) * tm_size + (tm_at + tm_step) % tm_size
            block = lax.dynamic_index_in_dim(blocks, target, 0, keepdims=False)
            if inp_step or tm_step:
                route = [
                    (g, ((g // tm_size + inp_step) % inp_size) * tm_size + (g % tm_size + tm_step) % tm_size)
                    for g in range(group_size)
                ]
                block = lax.ppermute(block, ("inp", "tm"), route)
            pieces.append(block)
    return pieces


def assemble_chunk(pieces, inp_at, inp_size, tm_size, cols):
    own_channels, _, spectra_here, inputs_here = pieces[0].shape
    half = jnp.zeros((own_channels, 2, tm_size, spectra_here, cols), jnp.bfloat16)
    for inp_step in range(inp_size):
        for tm_step in range(tm_size):
            block = pieces[inp_step * tm_size + tm_step]
            source_inp = (inp_at + inp_size - inp_step) % inp_size
            half = lax.dynamic_update_slice(
                half, block[:, :, None], (0, 0, tm_step, 0, source_inp * inputs_here)
            )
    return half


def finish_chunk(half, pol_size, cols):
    own_channels, _, tm_size, spectra_here, _ = half.shape
    if pol_size == 2:
        partner = lax.ppermute(half, "pol", [(0, 1), (1, 0)])
        both = jnp.stack([half, partner], axis=1)
    else:
        both = lax.all_gather(half, "pol", axis=1, tiled=False)
    depth = pol_size * 2 * tm_size * spectra_here
    left_all = both.reshape(own_channels, depth, cols)
    rows_here = cols // pol_size
    row_start = lax.axis_index("pol") * rows_here
    own_rows = lax.dynamic_slice_in_dim(both, row_start, rows_here, 5)
    swapped = jnp.stack([own_rows[:, :, 1], -own_rows[:, :, 0]], axis=2)
    lhs = jnp.stack([own_rows, swapped], axis=1).reshape(own_channels, 2, depth, rows_here)
    lhs = lhs.transpose(0, 1, 3, 2).reshape(own_channels, 2 * rows_here, depth)
    return lhs, left_all


def solution(mesh):
    return jax.shard_map(
        per_device,
        mesh=mesh,
        in_specs=(P(("group", "inp"), ("tm", "pol")),),
        out_specs=P(("group", "inp", "tm"), None, "pol", None),
        check_vma=False,
    )
```

```python
import functools
import math

import jax
import jax.numpy as jnp
from jax import lax
from jax.experimental import pallas as pl
from jax.sharding import PartitionSpec as P

CH = 512
TAPS = 16


def shifted(block, axis, distance):
    devices = range(lax.axis_size(axis))
    route = [(i - distance, i) for i in devices if i - distance in devices]
    return lax.ppermute(block, axis, route)


def prototype(tap_count, frame_len):
    length = tap_count * frame_len
    sample = lax.broadcasted_iota(jnp.int32, (length,), 0).astype(jnp.float32)
    centred = (sample - (length - 1) / 2.0) / frame_len
    window = 0.5 - 0.5 * jnp.cos(2.0 * math.pi * (sample + 0.5) / length)
    angle = math.pi * centred
    filter_taps = jnp.sin(angle) / angle * window
    filter_taps = filter_taps / jnp.sqrt(jnp.sum(filter_taps * filter_taps))
    return filter_taps.reshape(tap_count, frame_len)


def dft_table_t(frame_len):
    channel_idx = lax.broadcasted_iota(jnp.int32, (frame_len // 2, frame_len), 0)
    sample_idx = lax.broadcasted_iota(jnp.int32, (frame_len // 2, frame_len), 1)
    phase = (sample_idx * channel_idx % frame_len).astype(jnp.float32) * (2.0 * math.pi / frame_len)
    table = jnp.stack([jnp.cos(phase), -jnp.sin(phase)], axis=1)
    return table.reshape(frame_len, frame_len).astype(jnp.bfloat16)


def per_device(voltages):
    inputs_here = voltages.shape[0]
    frame_len = 2 * CH
    spectra_here = voltages.shape[1] // frame_len
    frames = voltages.reshape(inputs_here, spectra_here, frame_len).transpose(1, 0, 2)
    last_frames = frames[spectra_here - (TAPS - 1) :]
    filter_taps = prototype(TAPS, frame_len)
    table = dft_table_t(frame_len)
    quarters = 4
    width = frame_len // quarters
    spectra = None
    history = None
    for quarter in range(quarters):
        cut = slice(quarter * width, (quarter + 1) * width)
        last_part = last_frames[:, :, cut]
        if quarter:
            history, last_part = lax.optimization_barrier((history, last_part))
        history = shifted(last_part, ("tm", "pol"), 1)
        extended = jnp.concatenate([history, frames[:, :, cut]], axis=0)
        taps = filter_taps[:, cut]
        filtered = jnp.zeros((spectra_here, inputs_here, width), jnp.float32)
        for tap_index in range(TAPS):
            filtered = filtered + taps[tap_index] * extended[
                tap_index : tap_index + spectra_here
            ].astype(jnp.float32)
        filtered = filtered.astype(jnp.bfloat16)
        partial = lax.dot_general(
            table[:, cut],
            filtered.reshape(spectra_here * inputs_here, width),
            (((1,), (1,)), ((), ())),
            preferred_element_type=jnp.float32,
        )
        spectra = partial if spectra is None else spectra + partial
    spectra = spectra.astype(jnp.bfloat16).reshape(CH, 2, spectra_here, inputs_here)
    inp_size = lax.axis_size("inp")
    tm_size = lax.axis_size("tm")
    pol_size = lax.axis_size("pol")
    group_size = inp_size * tm_size
    own_channels = CH // group_size
    blocks = spectra.reshape(group_size, own_channels, 2, spectra_here, inputs_here)
    inp_at = lax.axis_index("inp")
    tm_at = lax.axis_index("tm")
    cols = inp_size * inputs_here
    chunks = 4 if own_channels % 8 == 0 else 1
    per_chunk = own_channels // chunks
    parts = [blocks[:, chunk * per_chunk : (chunk + 1) * per_chunk] for chunk in range(chunks)]
    out = None
    half = None
    for chunk in range(chunks):
        if chunk:
            half, parts[chunk] = lax.optimization_barrier((half, parts[chunk]))
        pieces = send_chunk(parts[chunk], inp_at, tm_at, inp_size, tm_size)
        if chunk:
            lhs, rhs = finish_chunk(half, pol_size, cols)
            out = correlate(lhs, rhs, out, (chunk - 1) * per_chunk, own_channels)
            out, pieces = lax.optimization_barrier((out, pieces))
        half = assemble_chunk(pieces, inp_at, inp_size, tm_size, cols)
    lhs, rhs = finish_chunk(half, pol_size, cols)
    return correlate(lhs, rhs, out, (chunks - 1) * per_chunk, own_channels)


def correlate_kernel(scale, lhs_ref, rhs_ref, *rest):
    out_ref = rest[-1]
    rows = out_ref.shape[2]
    for k in range(lhs_ref.shape[0]):
        acc = jnp.dot(lhs_ref[k], rhs_ref[k], preferred_element_type=jnp.float32) * scale
        out_ref[k, 0] = acc[:rows]
        out_ref[k, 1] = acc[rows:]


def correlate(lhs, rhs, prev, first_channel, own_channels):
    count, two_rows, depth = lhs.shape
    cols = rhs.shape[2]
    rows = two_rows // 2
    step = 2 if count % 2 == 0 else 1
    offset = first_channel // step
    in_specs = [
        pl.BlockSpec((step, two_rows, depth), lambda c: (c, 0, 0)),
        pl.BlockSpec((step, depth, cols), lambda c: (c, 0, 0)),
    ]
    args = [lhs, rhs]
    aliases = {}
    if prev is not None:
        in_specs.append(pl.BlockSpec(memory_space=pl.ANY))
        args.append(prev)
        aliases = {2: 0}
    flops = 2 * count * two_rows * depth * cols
    out_bytes = count * two_rows * cols * 4
    return pl.pallas_call(
        functools.partial(correlate_kernel, 1.0 / (depth // 2)),
        grid=(count // step,),
        in_specs=in_specs,
        out_specs=pl.BlockSpec((step, 2, rows, cols), lambda c: (c + offset, 0, 0, 0)),
        out_shape=jax.ShapeDtypeStruct((own_channels, 2, rows, cols), jnp.float32),
        input_output_aliases=aliases,
        cost_estimate=pl.CostEstimate(
            flops=flops, bytes_accessed=out_bytes + lhs.size * 2 + rhs.size * 2, transcendentals=0
        ),
    )(*args)


def send_chunk(blocks, inp_at, tm_at, inp_size, tm_size):
    group_size = blocks.shape[0]
    pieces = []
    for inp_step in range(inp_size):
        for tm_step in range(tm_size):
            target = ((inp_at + inp_step) % inp_size) * tm_size + (tm_at + tm_step) % tm_size
            block = lax.dynamic_index_in_dim(blocks, target, 0, keepdims=False)
            if inp_step or tm_step:
                route = [
                    (g, ((g // tm_size + inp_step) % inp_size) * tm_size + (g % tm_size + tm_step) % tm_size)
                    for g in range(group_size)
                ]
                block = lax.ppermute(block, ("inp", "tm"), route)
            pieces.append(block)
    return pieces


def assemble_chunk(pieces, inp_at, inp_size, tm_size, cols):
    own_channels, _, spectra_here, inputs_here = pieces[0].shape
    half = jnp.zeros((own_channels, 2, tm_size, spectra_here, cols), jnp.bfloat16)
    for inp_step in range(inp_size):
        for tm_step in range(tm_size):
            block = pieces[inp_step * tm_size + tm_step]
            source_inp = (inp_at + inp_size - inp_step) % inp_size
            half = lax.dynamic_update_slice(
                half, block[:, :, None], (0, 0, tm_step, 0, source_inp * inputs_here)
            )
    return half


def finish_chunk(half, pol_size, cols):
    own_channels, _, tm_size, spectra_here, _ = half.shape
    if pol_size == 2:
        partner = lax.ppermute(half, "pol", [(0, 1), (1, 0)])
        both = jnp.stack([half, partner], axis=1)
    else:
        both = lax.all_gather(half, "pol", axis=1, tiled=False)
    depth = pol_size * 2 * tm_size * spectra_here
    left_all = both.reshape(own_channels, depth, cols)
    rows_here = cols // pol_size
    row_start = lax.axis_index("pol") * rows_here
    own_rows = lax.dynamic_slice_in_dim(both, row_start, rows_here, 5)
    swapped = jnp.stack([own_rows[:, :, 1], -own_rows[:, :, 0]], axis=2)
    lhs = jnp.stack([own_rows, swapped], axis=1).reshape(own_channels, 2, depth, rows_here)
    lhs = lhs.transpose(0, 1, 3, 2).reshape(own_channels, 2 * rows_here, depth)
    return lhs, left_all


def solution(mesh):
    return jax.shard_map(
        per_device,
        mesh=mesh,
        in_specs=(P(("group", "inp"), ("tm", "pol")),),
        out_specs=P(("group", "inp", "tm"), None, "pol", None),
        check_vma=False,
    )
```

```python
import functools
import math

import jax
import jax.numpy as jnp
from jax import lax
from jax.experimental import pallas as pl
from jax.sharding import PartitionSpec as P

CH = 512
TAPS = 16


def shifted(block, axis, distance):
    devices = range(lax.axis_size(axis))
    route = [(i - distance, i) for i in devices if i - distance in devices]
    return lax.ppermute(block, axis, route)


def prototype(tap_count, frame_len):
    length = tap_count * frame_len
    sample = lax.broadcasted_iota(jnp.int32, (length,), 0).astype(jnp.float32)
    centred = (sample - (length - 1) / 2.0) / frame_len
    window = 0.5 - 0.5 * jnp.cos(2.0 * math.pi * (sample + 0.5) / length)
    angle = math.pi * centred
    filter_taps = jnp.sin(angle) / angle * window
    filter_taps = filter_taps / jnp.sqrt(jnp.sum(filter_taps * filter_taps))
    return filter_taps.reshape(tap_count, frame_len)


def dft_table_t(frame_len):
    channel_idx = lax.broadcasted_iota(jnp.int32, (frame_len // 2, frame_len), 0)
    sample_idx = lax.broadcasted_iota(jnp.int32, (frame_len // 2, frame_len), 1)
    phase = (sample_idx * channel_idx % frame_len).astype(jnp.float32) * (2.0 * math.pi / frame_len)
    table = jnp.stack([jnp.cos(phase), -jnp.sin(phase)], axis=1)
    return table.reshape(frame_len, frame_len).astype(jnp.bfloat16)


def per_device(voltages):
    inputs_here = voltages.shape[0]
    frame_len = 2 * CH
    spectra_here = voltages.shape[1] // frame_len
    frames = voltages.reshape(inputs_here, spectra_here, frame_len).transpose(1, 0, 2)
    last_frames = frames[spectra_here - (TAPS - 1) :]
    filter_taps = prototype(TAPS, frame_len)
    table = dft_table_t(frame_len)
    quarters = 4
    width = frame_len // quarters
    history = None
    filtered_all = jnp.zeros((spectra_here, inputs_here, frame_len), jnp.bfloat16)
    for quarter in range(quarters):
        cut = slice(quarter * width, (quarter + 1) * width)
        last_part = last_frames[:, :, cut]
        if quarter:
            history, last_part = lax.optimization_barrier((history, last_part))
        history = shifted(last_part, ("tm", "pol"), 1)
        extended = jnp.concatenate([history, frames[:, :, cut]], axis=0)
        taps = filter_taps[:, cut]
        filtered = jnp.zeros((spectra_here, inputs_here, width), jnp.float32)
        for tap_index in range(TAPS):
            filtered = filtered + taps[tap_index] * extended[
                tap_index : tap_index + spectra_here
            ].astype(jnp.float32)
        filtered_all = lax.dynamic_update_slice(
            filtered_all, filtered.astype(jnp.bfloat16), (0, 0, quarter * width)
        )
    spectra = lax.dot_general(
        table,
        filtered_all.reshape(spectra_here * inputs_here, frame_len),
        (((1,), (1,)), ((), ())),
        preferred_element_type=jnp.float32,
    )
    spectra = spectra.astype(jnp.bfloat16).reshape(CH, 2, spectra_here, inputs_here)
    inp_size = lax.axis_size("inp")
    tm_size = lax.axis_size("tm")
    pol_size = lax.axis_size("pol")
    group_size = inp_size * tm_size
    own_channels = CH // group_size
    blocks = spectra.reshape(group_size, own_channels, 2, spectra_here, inputs_here)
    inp_at = lax.axis_index("inp")
    tm_at = lax.axis_index("tm")
    cols = inp_size * inputs_here
    chunks = 4 if own_channels % 8 == 0 else 1
    per_chunk = own_channels // chunks
    parts = [blocks[:, chunk * per_chunk : (chunk + 1) * per_chunk] for chunk in range(chunks)]
    out = None
    half = None
    for chunk in range(chunks):
        if chunk:
            half, parts[chunk] = lax.optimization_barrier((half, parts[chunk]))
        pieces = send_chunk(parts[chunk], inp_at, tm_at, inp_size, tm_size)
        if chunk:
            lhs, rhs = finish_chunk(half, pol_size, cols)
            out = correlate(lhs, rhs, out, (chunk - 1) * per_chunk, own_channels)
            out, pieces = lax.optimization_barrier((out, pieces))
        half = assemble_chunk(pieces, inp_at, inp_size, tm_size, cols)
    lhs, rhs = finish_chunk(half, pol_size, cols)
    return correlate(lhs, rhs, out, (chunks - 1) * per_chunk, own_channels)


def correlate_kernel(scale, lhs_ref, rhs_ref, *rest):
    out_ref = rest[-1]
    rows = out_ref.shape[2]
    for k in range(lhs_ref.shape[0]):
        acc = jnp.dot(lhs_ref[k], rhs_ref[k], preferred_element_type=jnp.float32) * scale
        out_ref[k, 0] = acc[:rows]
        out_ref[k, 1] = acc[rows:]


def correlate(lhs, rhs, prev, first_channel, own_channels):
    count, two_rows, depth = lhs.shape
    cols = rhs.shape[2]
    rows = two_rows // 2
    step = 2 if count % 2 == 0 else 1
    offset = first_channel // step
    in_specs = [
        pl.BlockSpec((step, two_rows, depth), lambda c: (c, 0, 0)),
        pl.BlockSpec((step, depth, cols), lambda c: (c, 0, 0)),
    ]
    args = [lhs, rhs]
    aliases = {}
    if prev is not None:
        in_specs.append(pl.BlockSpec(memory_space=pl.ANY))
        args.append(prev)
        aliases = {2: 0}
    flops = 2 * count * two_rows * depth * cols
    out_bytes = count * two_rows * cols * 4
    return pl.pallas_call(
        functools.partial(correlate_kernel, 1.0 / (depth // 2)),
        grid=(count // step,),
        in_specs=in_specs,
        out_specs=pl.BlockSpec((step, 2, rows, cols), lambda c: (c + offset, 0, 0, 0)),
        out_shape=jax.ShapeDtypeStruct((own_channels, 2, rows, cols), jnp.float32),
        input_output_aliases=aliases,
        cost_estimate=pl.CostEstimate(
            flops=flops, bytes_accessed=out_bytes + lhs.size * 2 + rhs.size * 2, transcendentals=0
        ),
    )(*args)


def send_chunk(blocks, inp_at, tm_at, inp_size, tm_size):
    group_size = blocks.shape[0]
    pieces = []
    for inp_step in range(inp_size):
        for tm_step in range(tm_size):
            target = ((inp_at + inp_step) % inp_size) * tm_size + (tm_at + tm_step) % tm_size
            block = lax.dynamic_index_in_dim(blocks, target, 0, keepdims=False)
            if inp_step or tm_step:
                route = [
                    (g, ((g // tm_size + inp_step) % inp_size) * tm_size + (g % tm_size + tm_step) % tm_size)
                    for g in range(group_size)
                ]
                block = lax.ppermute(block, ("inp", "tm"), route)
            pieces.append(block)
    return pieces


def assemble_chunk(pieces, inp_at, inp_size, tm_size, cols):
    own_channels, _, spectra_here, inputs_here = pieces[0].shape
    half = jnp.zeros((own_channels, 2, tm_size, spectra_here, cols), jnp.bfloat16)
    for inp_step in range(inp_size):
        for tm_step in range(tm_size):
            block = pieces[inp_step * tm_size + tm_step]
            source_inp = (inp_at + inp_size - inp_step) % inp_size
            half = lax.dynamic_update_slice(
                half, block[:, :, None], (0, 0, tm_step, 0, source_inp * inputs_here)
            )
    return half


def finish_chunk(half, pol_size, cols):
    own_channels, _, tm_size, spectra_here, _ = half.shape
    if pol_size == 2:
        partner = lax.ppermute(half, "pol", [(0, 1), (1, 0)])
        both = jnp.stack([half, partner], axis=1)
    else:
        both = lax.all_gather(half, "pol", axis=1, tiled=False)
    depth = pol_size * 2 * tm_size * spectra_here
    left_all = both.reshape(own_channels, depth, cols)
    rows_here = cols // pol_size
    row_start = lax.axis_index("pol") * rows_here
    own_rows = lax.dynamic_slice_in_dim(both, row_start, rows_here, 5)
    swapped = jnp.stack([own_rows[:, :, 1], -own_rows[:, :, 0]], axis=2)
    lhs = jnp.stack([own_rows, swapped], axis=1).reshape(own_channels, 2, depth, rows_here)
    lhs = lhs.transpose(0, 1, 3, 2).reshape(own_channels, 2 * rows_here, depth)
    return lhs, left_all


def solution(mesh):
    return jax.shard_map(
        per_device,
        mesh=mesh,
        in_specs=(P(("group", "inp"), ("tm", "pol")),),
        out_specs=P(("group", "inp", "tm"), None, "pol", None),
        check_vma=False,
    )
```

```python
import functools
import math

import jax
import jax.numpy as jnp
from jax import lax
from jax.experimental import pallas as pl
from jax.sharding import PartitionSpec as P

CH = 512
TAPS = 16


def shifted(block, axis, distance):
    devices = range(lax.axis_size(axis))
    route = [(i - distance, i) for i in devices if i - distance in devices]
    return lax.ppermute(block, axis, route)


def prototype(tap_count, frame_len):
    length = tap_count * frame_len
    sample = lax.broadcasted_iota(jnp.int32, (length,), 0).astype(jnp.float32)
    centred = (sample - (length - 1) / 2.0) / frame_len
    window = 0.5 - 0.5 * jnp.cos(2.0 * math.pi * (sample + 0.5) / length)
    angle = math.pi * centred
    filter_taps = jnp.sin(angle) / angle * window
    filter_taps = filter_taps / jnp.sqrt(jnp.sum(filter_taps * filter_taps))
    return filter_taps.reshape(tap_count, frame_len)


def dft_table_t(frame_len):
    channel_idx = lax.broadcasted_iota(jnp.int32, (frame_len // 2, frame_len), 0)
    sample_idx = lax.broadcasted_iota(jnp.int32, (frame_len // 2, frame_len), 1)
    phase = (sample_idx * channel_idx % frame_len).astype(jnp.float32) * (2.0 * math.pi / frame_len)
    table = jnp.stack([jnp.cos(phase), -jnp.sin(phase)], axis=1)
    return table.reshape(frame_len, frame_len).astype(jnp.bfloat16)


def per_device(voltages):
    inputs_here = voltages.shape[0]
    frame_len = 2 * CH
    spectra_here = voltages.shape[1] // frame_len
    frames = voltages.reshape(inputs_here, spectra_here, frame_len).transpose(1, 0, 2)
    last_frames = frames[spectra_here - (TAPS - 1) :]
    history = shifted(last_frames, ("tm", "pol"), 1)
    extended = jnp.concatenate([history, frames], axis=0)
    filter_taps = prototype(TAPS, frame_len)
    filtered = jnp.zeros((spectra_here, inputs_here, frame_len), jnp.float32)
    for tap_index in range(TAPS):
        filtered = filtered + filter_taps[tap_index] * extended[
            tap_index : tap_index + spectra_here
        ].astype(jnp.float32)
    filtered = filtered.astype(jnp.bfloat16)
    spectra = lax.dot_general(
        dft_table_t(frame_len),
        filtered.reshape(spectra_here * inputs_here, frame_len),
        (((1,), (1,)), ((), ())),
        preferred_element_type=jnp.float32,
    )
    spectra = spectra.astype(jnp.bfloat16).reshape(CH, 2, spectra_here, inputs_here)
    inp_size = lax.axis_size("inp")
    tm_size = lax.axis_size("tm")
    pol_size = lax.axis_size("pol")
    group_size = inp_size * tm_size
    own_channels = CH // group_size
    blocks = spectra.reshape(group_size, own_channels, 2, spectra_here, inputs_here)
    inp_at = lax.axis_index("inp")
    tm_at = lax.axis_index("tm")
    cols = inp_size * inputs_here
    if own_channels % 8 == 0:
        eighth = own_channels // 8
        sizes = [3 * eighth, 2 * eighth, 2 * eighth, eighth]
    else:
        sizes = [own_channels]
    chunks = len(sizes)
    firsts = [sum(sizes[:chunk]) for chunk in range(chunks)]
    parts = [blocks[:, first : first + size] for first, size in zip(firsts, sizes)]
    out = None
    half = None
    for chunk in range(chunks):
        if chunk:
            half, parts[chunk] = lax.optimization_barrier((half, parts[chunk]))
        pieces = send_chunk(parts[chunk], inp_at, tm_at, inp_size, tm_size)
        if chunk:
            lhs, rhs = finish_chunk(half, pol_size, cols)
            out = correlate(lhs, rhs, out, firsts[chunk - 1], own_channels)
            out, pieces = lax.optimization_barrier((out, pieces))
        half = assemble_chunk(pieces, inp_at, inp_size, tm_size, cols)
    lhs, rhs = finish_chunk(half, pol_size, cols)
    return correlate(lhs, rhs, out, firsts[-1], own_channels)


def correlate_kernel(scale, lhs_ref, rhs_ref, *rest):
    out_ref = rest[-1]
    rows = out_ref.shape[2]
    for k in range(lhs_ref.shape[0]):
        acc = jnp.dot(lhs_ref[k], rhs_ref[k], preferred_element_type=jnp.float32) * scale
        out_ref[k, 0] = acc[:rows]
        out_ref[k, 1] = acc[rows:]


def correlate(lhs, rhs, prev, first_channel, own_channels):
    count, two_rows, depth = lhs.shape
    cols = rhs.shape[2]
    rows = two_rows // 2
    step = 2 if count % 2 == 0 else 1
    offset = first_channel // step
    in_specs = [
        pl.BlockSpec((step, two_rows, depth), lambda c: (c, 0, 0)),
        pl.BlockSpec((step, depth, cols), lambda c: (c, 0, 0)),
    ]
    args = [lhs, rhs]
    aliases = {}
    if prev is not None:
        in_specs.append(pl.BlockSpec(memory_space=pl.ANY))
        args.append(prev)
        aliases = {2: 0}
    flops = 2 * count * two_rows * depth * cols
    out_bytes = count * two_rows * cols * 4
    return pl.pallas_call(
        functools.partial(correlate_kernel, 1.0 / (depth // 2)),
        grid=(count // step,),
        in_specs=in_specs,
        out_specs=pl.BlockSpec((step, 2, rows, cols), lambda c: (c + offset, 0, 0, 0)),
        out_shape=jax.ShapeDtypeStruct((own_channels, 2, rows, cols), jnp.float32),
        input_output_aliases=aliases,
        cost_estimate=pl.CostEstimate(
            flops=flops, bytes_accessed=out_bytes + lhs.size * 2 + rhs.size * 2, transcendentals=0
        ),
    )(*args)


def send_chunk(blocks, inp_at, tm_at, inp_size, tm_size):
    group_size = blocks.shape[0]
    pieces = []
    for inp_step in range(inp_size):
        for tm_step in range(tm_size):
            target = ((inp_at + inp_step) % inp_size) * tm_size + (tm_at + tm_step) % tm_size
            block = lax.dynamic_index_in_dim(blocks, target, 0, keepdims=False)
            if inp_step or tm_step:
                route = [
                    (g, ((g // tm_size + inp_step) % inp_size) * tm_size + (g % tm_size + tm_step) % tm_size)
                    for g in range(group_size)
                ]
                block = lax.ppermute(block, ("inp", "tm"), route)
            pieces.append(block)
    return pieces


def assemble_chunk(pieces, inp_at, inp_size, tm_size, cols):
    own_channels, _, spectra_here, inputs_here = pieces[0].shape
    half = jnp.zeros((own_channels, 2, tm_size, spectra_here, cols), jnp.bfloat16)
    for inp_step in range(inp_size):
        for tm_step in range(tm_size):
            block = pieces[inp_step * tm_size + tm_step]
            source_inp = (inp_at + inp_size - inp_step) % inp_size
            half = lax.dynamic_update_slice(
                half, block[:, :, None], (0, 0, tm_step, 0, source_inp * inputs_here)
            )
    return half


def finish_chunk(half, pol_size, cols):
    own_channels, _, tm_size, spectra_here, _ = half.shape
    if pol_size == 2:
        partner = lax.ppermute(half, "pol", [(0, 1), (1, 0)])
        both = jnp.stack([half, partner], axis=1)
    else:
        both = lax.all_gather(half, "pol", axis=1, tiled=False)
    depth = pol_size * 2 * tm_size * spectra_here
    left_all = both.reshape(own_channels, depth, cols)
    rows_here = cols // pol_size
    row_start = lax.axis_index("pol") * rows_here
    own_rows = lax.dynamic_slice_in_dim(both, row_start, rows_here, 5)
    swapped = jnp.stack([own_rows[:, :, 1], -own_rows[:, :, 0]], axis=2)
    lhs = jnp.stack([own_rows, swapped], axis=1).reshape(own_channels, 2, depth, rows_here)
    lhs = lhs.transpose(0, 1, 3, 2).reshape(own_channels, 2 * rows_here, depth)
    return lhs, left_all


def solution(mesh):
    return jax.shard_map(
        per_device,
        mesh=mesh,
        in_specs=(P(("group", "inp"), ("tm", "pol")),),
        out_specs=P(("group", "inp", "tm"), None, "pol", None),
        check_vma=False,
    )
```

```python
import functools
import math

import jax
import jax.numpy as jnp
from jax import lax
from jax.experimental import pallas as pl
from jax.sharding import PartitionSpec as P

CH = 512
TAPS = 16


def shifted(block, axis, distance):
    devices = range(lax.axis_size(axis))
    route = [(i - distance, i) for i in devices if i - distance in devices]
    return lax.ppermute(block, axis, route)


def prototype(tap_count, frame_len):
    length = tap_count * frame_len
    sample = lax.broadcasted_iota(jnp.int32, (length,), 0).astype(jnp.float32)
    centred = (sample - (length - 1) / 2.0) / frame_len
    window = 0.5 - 0.5 * jnp.cos(2.0 * math.pi * (sample + 0.5) / length)
    angle = math.pi * centred
    filter_taps = jnp.sin(angle) / angle * window
    filter_taps = filter_taps / jnp.sqrt(jnp.sum(filter_taps * filter_taps))
    return filter_taps.reshape(tap_count, frame_len)


def dft_table_t(frame_len):
    channel_idx = lax.broadcasted_iota(jnp.int32, (frame_len // 2, frame_len), 0)
    sample_idx = lax.broadcasted_iota(jnp.int32, (frame_len // 2, frame_len), 1)
    phase = (sample_idx * channel_idx % frame_len).astype(jnp.float32) * (2.0 * math.pi / frame_len)
    table = jnp.stack([jnp.cos(phase), -jnp.sin(phase)], axis=1)
    return table.reshape(frame_len, frame_len).astype(jnp.bfloat16)


def copy_kernel(in_ref, out_ref):
    out_ref[0] = in_ref[...]


def split_frames(voltages, frame_len):
    inputs_here = voltages.shape[0]
    spectra_here = voltages.shape[1] // frame_len
    return pl.pallas_call(
        copy_kernel,
        grid=(spectra_here,),
        in_specs=[pl.BlockSpec((inputs_here, frame_len), lambda s: (0, s))],
        out_specs=pl.BlockSpec((1, inputs_here, frame_len), lambda s: (s, 0, 0)),
        out_shape=jax.ShapeDtypeStruct((spectra_here, inputs_here, frame_len), voltages.dtype),
        cost_estimate=pl.CostEstimate(flops=0, bytes_accessed=2 * voltages.size * 2, transcendentals=0),
    )(voltages)


def per_device(voltages):
    inputs_here = voltages.shape[0]
    frame_len = 2 * CH
    spectra_here = voltages.shape[1] // frame_len
    frames = split_frames(voltages, frame_len)
    last_frames = frames[spectra_here - (TAPS - 1) :]
    history = shifted(last_frames, ("tm", "pol"), 1)
    extended = jnp.concatenate([history, frames], axis=0)
    filter_taps = prototype(TAPS, frame_len)
    filtered = jnp.zeros((spectra_here, inputs_here, frame_len), jnp.float32)
    for tap_index in range(TAPS):
        filtered = filtered + filter_taps[tap_index] * extended[
            tap_index : tap_index + spectra_here
        ].astype(jnp.float32)
    filtered = filtered.astype(jnp.bfloat16)
    spectra = lax.dot_general(
        dft_table_t(frame_len),
        filtered.reshape(spectra_here * inputs_here, frame_len),
        (((1,), (1,)), ((), ())),
        preferred_element_type=jnp.float32,
    )
    spectra = spectra.astype(jnp.bfloat16).reshape(CH, 2, spectra_here, inputs_here)
    inp_size = lax.axis_size("inp")
    tm_size = lax.axis_size("tm")
    pol_size = lax.axis_size("pol")
    group_size = inp_size * tm_size
    own_channels = CH // group_size
    blocks = spectra.reshape(group_size, own_channels, 2, spectra_here, inputs_here)
    inp_at = lax.axis_index("inp")
    tm_at = lax.axis_index("tm")
    cols = inp_size * inputs_here
    chunks = 4 if own_channels % 8 == 0 else 1
    per_chunk = own_channels // chunks
    parts = [blocks[:, chunk * per_chunk : (chunk + 1) * per_chunk] for chunk in range(chunks)]
    out = None
    half = None
    for chunk in range(chunks):
        if chunk:
            half, parts[chunk] = lax.optimization_barrier((half, parts[chunk]))
        pieces = send_chunk(parts[chunk], inp_at, tm_at, inp_size, tm_size)
        if chunk:
            lhs, rhs = finish_chunk(half, pol_size, cols)
            out = correlate(lhs, rhs, out, (chunk - 1) * per_chunk, own_channels)
            out, pieces = lax.optimization_barrier((out, pieces))
        half = assemble_chunk(pieces, inp_at, inp_size, tm_size, cols)
    lhs, rhs = finish_chunk(half, pol_size, cols)
    return correlate(lhs, rhs, out, (chunks - 1) * per_chunk, own_channels)


def correlate_kernel(scale, lhs_ref, rhs_ref, *rest):
    out_ref = rest[-1]
    rows = out_ref.shape[2]
    for k in range(lhs_ref.shape[0]):
        acc = jnp.dot(lhs_ref[k], rhs_ref[k], preferred_element_type=jnp.float32) * scale
        out_ref[k, 0] = acc[:rows]
        out_ref[k, 1] = acc[rows:]


def correlate(lhs, rhs, prev, first_channel, own_channels):
    count, two_rows, depth = lhs.shape
    cols = rhs.shape[2]
    rows = two_rows // 2
    step = 2 if count % 2 == 0 else 1
    offset = first_channel // step
    in_specs = [
        pl.BlockSpec((step, two_rows, depth), lambda c: (c, 0, 0)),
        pl.BlockSpec((step, depth, cols), lambda c: (c, 0, 0)),
    ]
    args = [lhs, rhs]
    aliases = {}
    if prev is not None:
        in_specs.append(pl.BlockSpec(memory_space=pl.ANY))
        args.append(prev)
        aliases = {2: 0}
    flops = 2 * count * two_rows * depth * cols
    out_bytes = count * two_rows * cols * 4
    return pl.pallas_call(
        functools.partial(correlate_kernel, 1.0 / (depth // 2)),
        grid=(count // step,),
        in_specs=in_specs,
        out_specs=pl.BlockSpec((step, 2, rows, cols), lambda c: (c + offset, 0, 0, 0)),
        out_shape=jax.ShapeDtypeStruct((own_channels, 2, rows, cols), jnp.float32),
        input_output_aliases=aliases,
        cost_estimate=pl.CostEstimate(
            flops=flops, bytes_accessed=out_bytes + lhs.size * 2 + rhs.size * 2, transcendentals=0
        ),
    )(*args)


def send_chunk(blocks, inp_at, tm_at, inp_size, tm_size):
    group_size = blocks.shape[0]
    pieces = []
    for inp_step in range(inp_size):
        for tm_step in range(tm_size):
            target = ((inp_at + inp_step) % inp_size) * tm_size + (tm_at + tm_step) % tm_size
            block = lax.dynamic_index_in_dim(blocks, target, 0, keepdims=False)
            if inp_step or tm_step:
                route = [
                    (g, ((g // tm_size + inp_step) % inp_size) * tm_size + (g % tm_size + tm_step) % tm_size)
                    for g in range(group_size)
                ]
                block = lax.ppermute(block, ("inp", "tm"), route)
            pieces.append(block)
    return pieces


def assemble_chunk(pieces, inp_at, inp_size, tm_size, cols):
    own_channels, _, spectra_here, inputs_here = pieces[0].shape
    half = jnp.zeros((own_channels, 2, tm_size, spectra_here, cols), jnp.bfloat16)
    for inp_step in range(inp_size):
        for tm_step in range(tm_size):
            block = pieces[inp_step * tm_size + tm_step]
            source_inp = (inp_at + inp_size - inp_step) % inp_size
            half = lax.dynamic_update_slice(
                half, block[:, :, None], (0, 0, tm_step, 0, source_inp * inputs_here)
            )
    return half


def finish_chunk(half, pol_size, cols):
    own_channels, _, tm_size, spectra_here, _ = half.shape
    if pol_size == 2:
        partner = lax.ppermute(half, "pol", [(0, 1), (1, 0)])
        both = jnp.stack([half, partner], axis=1)
    else:
        both = lax.all_gather(half, "pol", axis=1, tiled=False)
    depth = pol_size * 2 * tm_size * spectra_here
    left_all = both.reshape(own_channels, depth, cols)
    rows_here = cols // pol_size
    row_start = lax.axis_index("pol") * rows_here
    own_rows = lax.dynamic_slice_in_dim(both, row_start, rows_here, 5)
    swapped = jnp.stack([own_rows[:, :, 1], -own_rows[:, :, 0]], axis=2)
    lhs = jnp.stack([own_rows, swapped], axis=1).reshape(own_channels, 2, depth, rows_here)
    lhs = lhs.transpose(0, 1, 3, 2).reshape(own_channels, 2 * rows_here, depth)
    return lhs, left_all


def solution(mesh):
    return jax.shard_map(
        per_device,
        mesh=mesh,
        in_specs=(P(("group", "inp"), ("tm", "pol")),),
        out_specs=P(("group", "inp", "tm"), None, "pol", None),
        check_vma=False,
    )
```

```python
import functools
import math

import jax
import jax.numpy as jnp
from jax import lax
from jax.experimental import pallas as pl
from jax.sharding import PartitionSpec as P

CH = 512
TAPS = 16


def shifted(block, axis, distance):
    devices = range(lax.axis_size(axis))
    route = [(i - distance, i) for i in devices if i - distance in devices]
    return lax.ppermute(block, axis, route)


def prototype(tap_count, frame_len):
    length = tap_count * frame_len
    sample = lax.broadcasted_iota(jnp.int32, (length,), 0).astype(jnp.float32)
    centred = (sample - (length - 1) / 2.0) / frame_len
    window = 0.5 - 0.5 * jnp.cos(2.0 * math.pi * (sample + 0.5) / length)
    angle = math.pi * centred
    filter_taps = jnp.sin(angle) / angle * window
    filter_taps = filter_taps / jnp.sqrt(jnp.sum(filter_taps * filter_taps))
    return filter_taps.reshape(tap_count, frame_len)


def dft_table_t(frame_len):
    channel_idx = lax.broadcasted_iota(jnp.int32, (frame_len // 2, frame_len), 0)
    sample_idx = lax.broadcasted_iota(jnp.int32, (frame_len // 2, frame_len), 1)
    phase = (sample_idx * channel_idx % frame_len).astype(jnp.float32) * (2.0 * math.pi / frame_len)
    table = jnp.stack([jnp.cos(phase), -jnp.sin(phase)], axis=1)
    return table.reshape(frame_len, frame_len).astype(jnp.bfloat16)


def per_device(voltages):
    inputs_here = voltages.shape[0]
    frame_len = 2 * CH
    spectra_here = voltages.shape[1] // frame_len
    history = shifted(voltages, ("tm", "pol"), 1)
    filter_taps = prototype(TAPS, frame_len)

    def frame(index):
        if index >= 0:
            return voltages[:, index * frame_len : (index + 1) * frame_len]
        index += spectra_here
        return history[:, index * frame_len : (index + 1) * frame_len]

    outputs = []
    for s in range(spectra_here):
        total = None
        for tap_index in range(TAPS):
            term = filter_taps[tap_index] * frame(s + tap_index - (TAPS - 1)).astype(jnp.float32)
            total = term if total is None else total + term
        outputs.append(total)
    filtered = jnp.stack(outputs).astype(jnp.bfloat16)
    spectra = lax.dot_general(
        dft_table_t(frame_len),
        filtered.reshape(spectra_here * inputs_here, frame_len),
        (((1,), (1,)), ((), ())),
        preferred_element_type=jnp.float32,
    )
    spectra = spectra.astype(jnp.bfloat16).reshape(CH, 2, spectra_here, inputs_here)
    inp_size = lax.axis_size("inp")
    tm_size = lax.axis_size("tm")
    pol_size = lax.axis_size("pol")
    group_size = inp_size * tm_size
    own_channels = CH // group_size
    blocks = spectra.reshape(group_size, own_channels, 2, spectra_here, inputs_here)
    inp_at = lax.axis_index("inp")
    tm_at = lax.axis_index("tm")
    cols = inp_size * inputs_here
    chunks = 4 if own_channels % 8 == 0 else 1
    per_chunk = own_channels // chunks
    parts = [blocks[:, chunk * per_chunk : (chunk + 1) * per_chunk] for chunk in range(chunks)]
    out = None
    half = None
    for chunk in range(chunks):
        if chunk:
            half, parts[chunk] = lax.optimization_barrier((half, parts[chunk]))
        pieces = send_chunk(parts[chunk], inp_at, tm_at, inp_size, tm_size)
        if chunk:
            lhs, rhs = finish_chunk(half, pol_size, cols)
            out = correlate(lhs, rhs, out, (chunk - 1) * per_chunk, own_channels)
            out, pieces = lax.optimization_barrier((out, pieces))
        half = assemble_chunk(pieces, inp_at, inp_size, tm_size, cols)
    lhs, rhs = finish_chunk(half, pol_size, cols)
    return correlate(lhs, rhs, out, (chunks - 1) * per_chunk, own_channels)


def correlate_kernel(scale, lhs_ref, rhs_ref, *rest):
    out_ref = rest[-1]
    rows = out_ref.shape[2]
    for k in range(lhs_ref.shape[0]):
        acc = jnp.dot(lhs_ref[k], rhs_ref[k], preferred_element_type=jnp.float32) * scale
        out_ref[k, 0] = acc[:rows]
        out_ref[k, 1] = acc[rows:]


def correlate(lhs, rhs, prev, first_channel, own_channels):
    count, two_rows, depth = lhs.shape
    cols = rhs.shape[2]
    rows = two_rows // 2
    step = 2 if count % 2 == 0 else 1
    offset = first_channel // step
    in_specs = [
        pl.BlockSpec((step, two_rows, depth), lambda c: (c, 0, 0)),
        pl.BlockSpec((step, depth, cols), lambda c: (c, 0, 0)),
    ]
    args = [lhs, rhs]
    aliases = {}
    if prev is not None:
        in_specs.append(pl.BlockSpec(memory_space=pl.ANY))
        args.append(prev)
        aliases = {2: 0}
    flops = 2 * count * two_rows * depth * cols
    out_bytes = count * two_rows * cols * 4
    return pl.pallas_call(
        functools.partial(correlate_kernel, 1.0 / (depth // 2)),
        grid=(count // step,),
        in_specs=in_specs,
        out_specs=pl.BlockSpec((step, 2, rows, cols), lambda c: (c + offset, 0, 0, 0)),
        out_shape=jax.ShapeDtypeStruct((own_channels, 2, rows, cols), jnp.float32),
        input_output_aliases=aliases,
        cost_estimate=pl.CostEstimate(
            flops=flops, bytes_accessed=out_bytes + lhs.size * 2 + rhs.size * 2, transcendentals=0
        ),
    )(*args)


def send_chunk(blocks, inp_at, tm_at, inp_size, tm_size):
    group_size = blocks.shape[0]
    pieces = []
    for inp_step in range(inp_size):
        for tm_step in range(tm_size):
            target = ((inp_at + inp_step) % inp_size) * tm_size + (tm_at + tm_step) % tm_size
            block = lax.dynamic_index_in_dim(blocks, target, 0, keepdims=False)
            if inp_step or tm_step:
                route = [
                    (g, ((g // tm_size + inp_step) % inp_size) * tm_size + (g % tm_size + tm_step) % tm_size)
                    for g in range(group_size)
                ]
                block = lax.ppermute(block, ("inp", "tm"), route)
            pieces.append(block)
    return pieces


def assemble_chunk(pieces, inp_at, inp_size, tm_size, cols):
    own_channels, _, spectra_here, inputs_here = pieces[0].shape
    half = jnp.zeros((own_channels, 2, tm_size, spectra_here, cols), jnp.bfloat16)
    for inp_step in range(inp_size):
        for tm_step in range(tm_size):
            block = pieces[inp_step * tm_size + tm_step]
            source_inp = (inp_at + inp_size - inp_step) % inp_size
            half = lax.dynamic_update_slice(
                half, block[:, :, None], (0, 0, tm_step, 0, source_inp * inputs_here)
            )
    return half


def finish_chunk(half, pol_size, cols):
    own_channels, _, tm_size, spectra_here, _ = half.shape
    if pol_size == 2:
        partner = lax.ppermute(half, "pol", [(0, 1), (1, 0)])
        both = jnp.stack([half, partner], axis=1)
    else:
        both = lax.all_gather(half, "pol", axis=1, tiled=False)
    depth = pol_size * 2 * tm_size * spectra_here
    left_all = both.reshape(own_channels, depth, cols)
    rows_here = cols // pol_size
    row_start = lax.axis_index("pol") * rows_here
    own_rows = lax.dynamic_slice_in_dim(both, row_start, rows_here, 5)
    swapped = jnp.stack([own_rows[:, :, 1], -own_rows[:, :, 0]], axis=2)
    lhs = jnp.stack([own_rows, swapped], axis=1).reshape(own_channels, 2, depth, rows_here)
    lhs = lhs.transpose(0, 1, 3, 2).reshape(own_channels, 2 * rows_here, depth)
    return lhs, left_all


def solution(mesh):
    return jax.shard_map(
        per_device,
        mesh=mesh,
        in_specs=(P(("group", "inp"), ("tm", "pol")),),
        out_specs=P(("group", "inp", "tm"), None, "pol", None),
        check_vma=False,
    )
```

```python
import functools
import math

import jax
import jax.numpy as jnp
from jax import lax
from jax.experimental import pallas as pl
from jax.sharding import PartitionSpec as P

CH = 512
TAPS = 16


def shifted(block, axis, distance):
    devices = range(lax.axis_size(axis))
    route = [(i - distance, i) for i in devices if i - distance in devices]
    return lax.ppermute(block, axis, route)


def prototype(tap_count, frame_len):
    length = tap_count * frame_len
    sample = lax.broadcasted_iota(jnp.int32, (length,), 0).astype(jnp.float32)
    centred = (sample - (length - 1) / 2.0) / frame_len
    window = 0.5 - 0.5 * jnp.cos(2.0 * math.pi * (sample + 0.5) / length)
    angle = math.pi * centred
    filter_taps = jnp.sin(angle) / angle * window
    filter_taps = filter_taps / jnp.sqrt(jnp.sum(filter_taps * filter_taps))
    return filter_taps.reshape(tap_count, frame_len)


def dft_table_t(frame_len):
    channel_idx = lax.broadcasted_iota(jnp.int32, (frame_len // 2, frame_len), 0)
    sample_idx = lax.broadcasted_iota(jnp.int32, (frame_len // 2, frame_len), 1)
    phase = (sample_idx * channel_idx % frame_len).astype(jnp.float32) * (2.0 * math.pi / frame_len)
    table = jnp.stack([jnp.cos(phase), -jnp.sin(phase)], axis=1)
    return table.reshape(frame_len, frame_len).astype(jnp.bfloat16)


def filter_kernel(taps_ref, own_ref, history_ref, out_ref):
    spectra_here, inputs_here, frame_len = out_ref.shape
    tile_rows, tile_cols = 16, 128
    col_tiles = frame_len // tile_cols

    def body(tile, carry):
        r0 = pl.multiple_of((tile // col_tiles) * tile_rows, tile_rows)
        c0 = pl.multiple_of((tile % col_tiles) * tile_cols, tile_cols)
        taps = [taps_ref[k : k + 1, pl.ds(c0, tile_cols)] for k in range(TAPS)]
        sums = [None] * spectra_here
        for j in range(spectra_here + TAPS - 1):
            if j < TAPS - 1:
                col = (spectra_here - (TAPS - 1) + j) * frame_len
                block = history_ref[pl.ds(r0, tile_rows), pl.ds(col + c0, tile_cols)]
            else:
                col = (j - (TAPS - 1)) * frame_len
                block = own_ref[pl.ds(r0, tile_rows), pl.ds(col + c0, tile_cols)]
            block = block.astype(jnp.float32)
            for s in range(max(0, j - (TAPS - 1)), min(spectra_here - 1, j) + 1):
                term = taps[j - s] * block
                sums[s] = term if sums[s] is None else sums[s] + term
        for s in range(spectra_here):
            out_ref[s, pl.ds(r0, tile_rows), pl.ds(c0, tile_cols)] = sums[s].astype(out_ref.dtype)
        return carry

    lax.fori_loop(0, (inputs_here // tile_rows) * col_tiles, body, 0)


def polyphase_filter(filter_taps, own, history, frame_len):
    inputs_here = own.shape[0]
    spectra_here = own.shape[1] // frame_len
    return pl.pallas_call(
        filter_kernel,
        out_shape=jax.ShapeDtypeStruct((spectra_here, inputs_here, frame_len), jnp.bfloat16),
        cost_estimate=pl.CostEstimate(
            flops=2 * TAPS * own.size, bytes_accessed=3 * own.size * 2, transcendentals=0
        ),
    )(filter_taps, own, history)


def per_device(voltages):
    inputs_here = voltages.shape[0]
    frame_len = 2 * CH
    spectra_here = voltages.shape[1] // frame_len
    history = shifted(voltages, ("tm", "pol"), 1)
    filtered = polyphase_filter(prototype(TAPS, frame_len), voltages, history, frame_len)
    spectra = lax.dot_general(
        dft_table_t(frame_len),
        filtered.reshape(spectra_here * inputs_here, frame_len),
        (((1,), (1,)), ((), ())),
        preferred_element_type=jnp.float32,
    )
    spectra = spectra.astype(jnp.bfloat16).reshape(CH, 2, spectra_here, inputs_here)
    inp_size = lax.axis_size("inp")
    tm_size = lax.axis_size("tm")
    pol_size = lax.axis_size("pol")
    group_size = inp_size * tm_size
    own_channels = CH // group_size
    blocks = spectra.reshape(group_size, own_channels, 2, spectra_here, inputs_here)
    inp_at = lax.axis_index("inp")
    tm_at = lax.axis_index("tm")
    cols = inp_size * inputs_here
    chunks = 4 if own_channels % 8 == 0 else 1
    per_chunk = own_channels // chunks
    parts = [blocks[:, chunk * per_chunk : (chunk + 1) * per_chunk] for chunk in range(chunks)]
    out = None
    half = None
    for chunk in range(chunks):
        if chunk:
            half, parts[chunk] = lax.optimization_barrier((half, parts[chunk]))
        pieces = send_chunk(parts[chunk], inp_at, tm_at, inp_size, tm_size)
        if chunk:
            lhs, rhs = finish_chunk(half, pol_size, cols)
            out = correlate(lhs, rhs, out, (chunk - 1) * per_chunk, own_channels)
            out, pieces = lax.optimization_barrier((out, pieces))
        half = assemble_chunk(pieces, inp_at, inp_size, tm_size, cols)
    lhs, rhs = finish_chunk(half, pol_size, cols)
    return correlate(lhs, rhs, out, (chunks - 1) * per_chunk, own_channels)


def correlate_kernel(scale, lhs_ref, rhs_ref, *rest):
    out_ref = rest[-1]
    rows = out_ref.shape[2]
    for k in range(lhs_ref.shape[0]):
        acc = jnp.dot(lhs_ref[k], rhs_ref[k], preferred_element_type=jnp.float32) * scale
        out_ref[k, 0] = acc[:rows]
        out_ref[k, 1] = acc[rows:]


def correlate(lhs, rhs, prev, first_channel, own_channels):
    count, two_rows, depth = lhs.shape
    cols = rhs.shape[2]
    rows = two_rows // 2
    step = 2 if count % 2 == 0 else 1
    offset = first_channel // step
    in_specs = [
        pl.BlockSpec((step, two_rows, depth), lambda c: (c, 0, 0)),
        pl.BlockSpec((step, depth, cols), lambda c: (c, 0, 0)),
    ]
    args = [lhs, rhs]
    aliases = {}
    if prev is not None:
        in_specs.append(pl.BlockSpec(memory_space=pl.ANY))
        args.append(prev)
        aliases = {2: 0}
    flops = 2 * count * two_rows * depth * cols
    out_bytes = count * two_rows * cols * 4
    return pl.pallas_call(
        functools.partial(correlate_kernel, 1.0 / (depth // 2)),
        grid=(count // step,),
        in_specs=in_specs,
        out_specs=pl.BlockSpec((step, 2, rows, cols), lambda c: (c + offset, 0, 0, 0)),
        out_shape=jax.ShapeDtypeStruct((own_channels, 2, rows, cols), jnp.float32),
        input_output_aliases=aliases,
        cost_estimate=pl.CostEstimate(
            flops=flops, bytes_accessed=out_bytes + lhs.size * 2 + rhs.size * 2, transcendentals=0
        ),
    )(*args)


def send_chunk(blocks, inp_at, tm_at, inp_size, tm_size):
    group_size = blocks.shape[0]
    pieces = []
    for inp_step in range(inp_size):
        for tm_step in range(tm_size):
            target = ((inp_at + inp_step) % inp_size) * tm_size + (tm_at + tm_step) % tm_size
            block = lax.dynamic_index_in_dim(blocks, target, 0, keepdims=False)
            if inp_step or tm_step:
                route = [
                    (g, ((g // tm_size + inp_step) % inp_size) * tm_size + (g % tm_size + tm_step) % tm_size)
                    for g in range(group_size)
                ]
                block = lax.ppermute(block, ("inp", "tm"), route)
            pieces.append(block)
    return pieces


def assemble_chunk(pieces, inp_at, inp_size, tm_size, cols):
    own_channels, _, spectra_here, inputs_here = pieces[0].shape
    half = jnp.zeros((own_channels, 2, tm_size, spectra_here, cols), jnp.bfloat16)
    for inp_step in range(inp_size):
        for tm_step in range(tm_size):
            block = pieces[inp_step * tm_size + tm_step]
            source_inp = (inp_at + inp_size - inp_step) % inp_size
            half = lax.dynamic_update_slice(
                half, block[:, :, None], (0, 0, tm_step, 0, source_inp * inputs_here)
            )
    return half


def finish_chunk(half, pol_size, cols):
    own_channels, _, tm_size, spectra_here, _ = half.shape
    if pol_size == 2:
        partner = lax.ppermute(half, "pol", [(0, 1), (1, 0)])
        both = jnp.stack([half, partner], axis=1)
    else:
        both = lax.all_gather(half, "pol", axis=1, tiled=False)
    depth = pol_size * 2 * tm_size * spectra_here
    left_all = both.reshape(own_channels, depth, cols)
    rows_here = cols // pol_size
    row_start = lax.axis_index("pol") * rows_here
    own_rows = lax.dynamic_slice_in_dim(both, row_start, rows_here, 5)
    swapped = jnp.stack([own_rows[:, :, 1], -own_rows[:, :, 0]], axis=2)
    lhs = jnp.stack([own_rows, swapped], axis=1).reshape(own_channels, 2, depth, rows_here)
    lhs = lhs.transpose(0, 1, 3, 2).reshape(own_channels, 2 * rows_here, depth)
    return lhs, left_all


def solution(mesh):
    return jax.shard_map(
        per_device,
        mesh=mesh,
        in_specs=(P(("group", "inp"), ("tm", "pol")),),
        out_specs=P(("group", "inp", "tm"), None, "pol", None),
        check_vma=False,
    )
```

```python
import functools
import math

import jax
import jax.numpy as jnp
from jax import lax
from jax.experimental import pallas as pl
from jax.sharding import PartitionSpec as P

CH = 512
TAPS = 16


def shifted(block, axis, distance):
    devices = range(lax.axis_size(axis))
    route = [(i - distance, i) for i in devices if i - distance in devices]
    return lax.ppermute(block, axis, route)


def prototype(tap_count, frame_len):
    length = tap_count * frame_len
    sample = lax.broadcasted_iota(jnp.int32, (length,), 0).astype(jnp.float32)
    centred = (sample - (length - 1) / 2.0) / frame_len
    window = 0.5 - 0.5 * jnp.cos(2.0 * math.pi * (sample + 0.5) / length)
    angle = math.pi * centred
    filter_taps = jnp.sin(angle) / angle * window
    filter_taps = filter_taps / jnp.sqrt(jnp.sum(filter_taps * filter_taps))
    return filter_taps.reshape(tap_count, frame_len)


def dft_table_t(frame_len):
    channel_idx = lax.broadcasted_iota(jnp.int32, (frame_len // 2, frame_len), 0)
    sample_idx = lax.broadcasted_iota(jnp.int32, (frame_len // 2, frame_len), 1)
    phase = (sample_idx * channel_idx % frame_len).astype(jnp.float32) * (2.0 * math.pi / frame_len)
    table = jnp.stack([jnp.cos(phase), -jnp.sin(phase)], axis=1)
    return table.reshape(frame_len, frame_len).astype(jnp.bfloat16)


def filter_kernel(taps_ref, own_ref, history_ref, out_ref):
    spectra_here, inputs_here, frame_len = out_ref.shape
    tile_rows, tile_cols = 16, 128
    col_tiles = frame_len // tile_cols

    def body(tile, carry):
        r0 = pl.multiple_of((tile // col_tiles) * tile_rows, tile_rows)
        c0 = pl.multiple_of((tile % col_tiles) * tile_cols, tile_cols)
        taps = [taps_ref[k : k + 1, pl.ds(c0, tile_cols)] for k in range(TAPS)]
        sums = [None] * spectra_here
        for j in range(spectra_here + TAPS - 1):
            if j < TAPS - 1:
                col = (spectra_here - (TAPS - 1) + j) * frame_len
                block = history_ref[pl.ds(r0, tile_rows), pl.ds(col + c0, tile_cols)]
            else:
                col = (j - (TAPS - 1)) * frame_len
                block = own_ref[pl.ds(r0, tile_rows), pl.ds(col + c0, tile_cols)]
            block = block.astype(jnp.float32)
            for s in range(max(0, j - (TAPS - 1)), min(spectra_here - 1, j) + 1):
                term = taps[j - s] * block
                sums[s] = term if sums[s] is None else sums[s] + term
        for s in range(spectra_here):
            out_ref[s, pl.ds(r0, tile_rows), pl.ds(c0, tile_cols)] = sums[s].astype(out_ref.dtype)
        return carry

    lax.fori_loop(0, (inputs_here // tile_rows) * col_tiles, body, 0)


def polyphase_filter(filter_taps, own, history, frame_len):
    inputs_here = own.shape[0]
    spectra_here = own.shape[1] // frame_len
    rows = 32 if inputs_here % 32 == 0 else inputs_here
    return pl.pallas_call(
        filter_kernel,
        grid=(inputs_here // rows,),
        in_specs=[
            pl.BlockSpec((TAPS, frame_len), lambda r: (0, 0)),
            pl.BlockSpec((rows, spectra_here * frame_len), lambda r: (r, 0)),
            pl.BlockSpec((rows, spectra_here * frame_len), lambda r: (r, 0)),
        ],
        out_specs=pl.BlockSpec((spectra_here, rows, frame_len), lambda r: (0, r, 0)),
        out_shape=jax.ShapeDtypeStruct((spectra_here, inputs_here, frame_len), jnp.bfloat16),
        cost_estimate=pl.CostEstimate(
            flops=2 * TAPS * own.size, bytes_accessed=3 * own.size * 2, transcendentals=0
        ),
    )(filter_taps, own, history)


def per_device(voltages):
    inputs_here = voltages.shape[0]
    frame_len = 2 * CH
    spectra_here = voltages.shape[1] // frame_len
    history = shifted(voltages, ("tm", "pol"), 1)
    filtered = polyphase_filter(prototype(TAPS, frame_len), voltages, history, frame_len)
    spectra = lax.dot_general(
        dft_table_t(frame_len),
        filtered.reshape(spectra_here * inputs_here, frame_len),
        (((1,), (1,)), ((), ())),
        preferred_element_type=jnp.float32,
    )
    spectra = spectra.astype(jnp.bfloat16).reshape(CH, 2, spectra_here, inputs_here)
    inp_size = lax.axis_size("inp")
    tm_size = lax.axis_size("tm")
    pol_size = lax.axis_size("pol")
    group_size = inp_size * tm_size
    own_channels = CH // group_size
    blocks = spectra.reshape(group_size, own_channels, 2, spectra_here, inputs_here)
    inp_at = lax.axis_index("inp")
    tm_at = lax.axis_index("tm")
    cols = inp_size * inputs_here
    chunks = 4 if own_channels % 8 == 0 else 1
    per_chunk = own_channels // chunks
    parts = [blocks[:, chunk * per_chunk : (chunk + 1) * per_chunk] for chunk in range(chunks)]
    out = None
    half = None
    for chunk in range(chunks):
        if chunk:
            half, parts[chunk] = lax.optimization_barrier((half, parts[chunk]))
        pieces = send_chunk(parts[chunk], inp_at, tm_at, inp_size, tm_size)
        if chunk:
            lhs, rhs = finish_chunk(half, pol_size, cols)
            out = correlate(lhs, rhs, out, (chunk - 1) * per_chunk, own_channels)
            out, pieces = lax.optimization_barrier((out, pieces))
        half = assemble_chunk(pieces, inp_at, inp_size, tm_size, cols)
    lhs, rhs = finish_chunk(half, pol_size, cols)
    return correlate(lhs, rhs, out, (chunks - 1) * per_chunk, own_channels)


def correlate_kernel(scale, lhs_ref, rhs_ref, *rest):
    out_ref = rest[-1]
    rows = out_ref.shape[2]
    for k in range(lhs_ref.shape[0]):
        acc = jnp.dot(lhs_ref[k], rhs_ref[k], preferred_element_type=jnp.float32) * scale
        out_ref[k, 0] = acc[:rows]
        out_ref[k, 1] = acc[rows:]


def correlate(lhs, rhs, prev, first_channel, own_channels):
    count, two_rows, depth = lhs.shape
    cols = rhs.shape[2]
    rows = two_rows // 2
    step = 2 if count % 2 == 0 else 1
    offset = first_channel // step
    in_specs = [
        pl.BlockSpec((step, two_rows, depth), lambda c: (c, 0, 0)),
        pl.BlockSpec((step, depth, cols), lambda c: (c, 0, 0)),
    ]
    args = [lhs, rhs]
    aliases = {}
    if prev is not None:
        in_specs.append(pl.BlockSpec(memory_space=pl.ANY))
        args.append(prev)
        aliases = {2: 0}
    flops = 2 * count * two_rows * depth * cols
    out_bytes = count * two_rows * cols * 4
    return pl.pallas_call(
        functools.partial(correlate_kernel, 1.0 / (depth // 2)),
        grid=(count // step,),
        in_specs=in_specs,
        out_specs=pl.BlockSpec((step, 2, rows, cols), lambda c: (c + offset, 0, 0, 0)),
        out_shape=jax.ShapeDtypeStruct((own_channels, 2, rows, cols), jnp.float32),
        input_output_aliases=aliases,
        cost_estimate=pl.CostEstimate(
            flops=flops, bytes_accessed=out_bytes + lhs.size * 2 + rhs.size * 2, transcendentals=0
        ),
    )(*args)


def send_chunk(blocks, inp_at, tm_at, inp_size, tm_size):
    group_size = blocks.shape[0]
    pieces = []
    for inp_step in range(inp_size):
        for tm_step in range(tm_size):
            target = ((inp_at + inp_step) % inp_size) * tm_size + (tm_at + tm_step) % tm_size
            block = lax.dynamic_index_in_dim(blocks, target, 0, keepdims=False)
            if inp_step or tm_step:
                route = [
                    (g, ((g // tm_size + inp_step) % inp_size) * tm_size + (g % tm_size + tm_step) % tm_size)
                    for g in range(group_size)
                ]
                block = lax.ppermute(block, ("inp", "tm"), route)
            pieces.append(block)
    return pieces


def assemble_chunk(pieces, inp_at, inp_size, tm_size, cols):
    own_channels, _, spectra_here, inputs_here = pieces[0].shape
    half = jnp.zeros((own_channels, 2, tm_size, spectra_here, cols), jnp.bfloat16)
    for inp_step in range(inp_size):
        for tm_step in range(tm_size):
            block = pieces[inp_step * tm_size + tm_step]
            source_inp = (inp_at + inp_size - inp_step) % inp_size
            half = lax.dynamic_update_slice(
                half, block[:, :, None], (0, 0, tm_step, 0, source_inp * inputs_here)
            )
    return half


def finish_chunk(half, pol_size, cols):
    own_channels, _, tm_size, spectra_here, _ = half.shape
    if pol_size == 2:
        partner = lax.ppermute(half, "pol", [(0, 1), (1, 0)])
        both = jnp.stack([half, partner], axis=1)
    else:
        both = lax.all_gather(half, "pol", axis=1, tiled=False)
    depth = pol_size * 2 * tm_size * spectra_here
    left_all = both.reshape(own_channels, depth, cols)
    rows_here = cols // pol_size
    row_start = lax.axis_index("pol") * rows_here
    own_rows = lax.dynamic_slice_in_dim(both, row_start, rows_here, 5)
    swapped = jnp.stack([own_rows[:, :, 1], -own_rows[:, :, 0]], axis=2)
    lhs = jnp.stack([own_rows, swapped], axis=1).reshape(own_channels, 2, depth, rows_here)
    lhs = lhs.transpose(0, 1, 3, 2).reshape(own_channels, 2 * rows_here, depth)
    return lhs, left_all


def solution(mesh):
    return jax.shard_map(
        per_device,
        mesh=mesh,
        in_specs=(P(("group", "inp"), ("tm", "pol")),),
        out_specs=P(("group", "inp", "tm"), None, "pol", None),
        check_vma=False,
    )
```

```python
import functools
import math

import jax
import jax.numpy as jnp
from jax import lax
from jax.experimental import pallas as pl
from jax.sharding import PartitionSpec as P

CH = 512
TAPS = 16


def shifted(block, axis, distance):
    devices = range(lax.axis_size(axis))
    route = [(i - distance, i) for i in devices if i - distance in devices]
    return lax.ppermute(block, axis, route)


def prototype(tap_count, frame_len):
    length = tap_count * frame_len
    sample = lax.broadcasted_iota(jnp.int32, (length,), 0).astype(jnp.float32)
    centred = (sample - (length - 1) / 2.0) / frame_len
    window = 0.5 - 0.5 * jnp.cos(2.0 * math.pi * (sample + 0.5) / length)
    angle = math.pi * centred
    filter_taps = jnp.sin(angle) / angle * window
    filter_taps = filter_taps / jnp.sqrt(jnp.sum(filter_taps * filter_taps))
    return filter_taps.reshape(tap_count, frame_len)


def dft_table_t(frame_len):
    channel_idx = lax.broadcasted_iota(jnp.int32, (frame_len // 2, frame_len), 0)
    sample_idx = lax.broadcasted_iota(jnp.int32, (frame_len // 2, frame_len), 1)
    phase = (sample_idx * channel_idx % frame_len).astype(jnp.float32) * (2.0 * math.pi / frame_len)
    table = jnp.stack([jnp.cos(phase), -jnp.sin(phase)], axis=1)
    return table.reshape(frame_len, frame_len).astype(jnp.bfloat16)


def filter_kernel(taps_ref, own_ref, history_ref, *rest):
    out_ref = rest[-1]
    spectra_here, inputs_here, frame_len = out_ref.shape
    tile_rows, tile_cols = 16, 128
    col_tiles = frame_len // tile_cols

    def body(tile, carry):
        r0 = pl.multiple_of((tile // col_tiles) * tile_rows, tile_rows)
        c0 = pl.multiple_of((tile % col_tiles) * tile_cols, tile_cols)
        taps = [taps_ref[k : k + 1, pl.ds(c0, tile_cols)] for k in range(TAPS)]
        sums = [None] * spectra_here
        for j in range(spectra_here + TAPS - 1):
            if j < TAPS - 1:
                col = (spectra_here - (TAPS - 1) + j) * frame_len
                block = history_ref[pl.ds(r0, tile_rows), pl.ds(col + c0, tile_cols)]
            else:
                col = (j - (TAPS - 1)) * frame_len
                block = own_ref[pl.ds(r0, tile_rows), pl.ds(col + c0, tile_cols)]
            block = block.astype(jnp.float32)
            for s in range(max(0, j - (TAPS - 1)), min(spectra_here - 1, j) + 1):
                term = taps[j - s] * block
                sums[s] = term if sums[s] is None else sums[s] + term
        for s in range(spectra_here):
            out_ref[s, pl.ds(r0, tile_rows), pl.ds(c0, tile_cols)] = sums[s].astype(out_ref.dtype)
        return carry

    lax.fori_loop(0, (inputs_here // tile_rows) * col_tiles, body, 0)


def polyphase_filter(filter_taps, own, history, frame_len, prev, part, inputs_total):
    inputs_here = own.shape[0]
    spectra_here = own.shape[1] // frame_len
    rows = 32 if inputs_here % 32 == 0 else inputs_here
    offset = part * (inputs_here // rows)
    in_specs = [
        pl.BlockSpec((TAPS, frame_len), lambda r: (0, 0)),
        pl.BlockSpec((rows, spectra_here * frame_len), lambda r: (r, 0)),
        pl.BlockSpec((rows, spectra_here * frame_len), lambda r: (r, 0)),
    ]
    args = [filter_taps, own, history]
    aliases = {}
    if prev is not None:
        in_specs.append(pl.BlockSpec(memory_space=pl.ANY))
        args.append(prev)
        aliases = {3: 0}
    return pl.pallas_call(
        filter_kernel,
        grid=(inputs_here // rows,),
        in_specs=in_specs,
        out_specs=pl.BlockSpec((spectra_here, rows, frame_len), lambda r: (0, r + offset, 0)),
        out_shape=jax.ShapeDtypeStruct((spectra_here, inputs_total, frame_len), jnp.bfloat16),
        input_output_aliases=aliases,
        cost_estimate=pl.CostEstimate(
            flops=2 * TAPS * own.size, bytes_accessed=3 * own.size * 2, transcendentals=0
        ),
    )(*args)


def per_device(voltages):
    inputs_here = voltages.shape[0]
    frame_len = 2 * CH
    spectra_here = voltages.shape[1] // frame_len
    filter_taps = prototype(TAPS, frame_len)
    halves = 2 if inputs_here % 64 == 0 else 1
    half_rows = inputs_here // halves
    filtered = None
    history = None
    for half in range(halves):
        rows = voltages[half * half_rows : (half + 1) * half_rows]
        if half:
            history, rows = lax.optimization_barrier((history, rows))
        history = shifted(rows, ("tm", "pol"), 1)
        filtered = polyphase_filter(filter_taps, rows, history, frame_len, filtered, half, inputs_here)
    spectra = lax.dot_general(
        dft_table_t(frame_len),
        filtered.reshape(spectra_here * inputs_here, frame_len),
        (((1,), (1,)), ((), ())),
        preferred_element_type=jnp.float32,
    )
    spectra = spectra.astype(jnp.bfloat16).reshape(CH, 2, spectra_here, inputs_here)
    inp_size = lax.axis_size("inp")
    tm_size = lax.axis_size("tm")
    pol_size = lax.axis_size("pol")
    group_size = inp_size * tm_size
    own_channels = CH // group_size
    blocks = spectra.reshape(group_size, own_channels, 2, spectra_here, inputs_here)
    inp_at = lax.axis_index("inp")
    tm_at = lax.axis_index("tm")
    cols = inp_size * inputs_here
    chunks = 4 if own_channels % 8 == 0 else 1
    per_chunk = own_channels // chunks
    parts = [blocks[:, chunk * per_chunk : (chunk + 1) * per_chunk] for chunk in range(chunks)]
    out = None
    half = None
    for chunk in range(chunks):
        if chunk:
            half, parts[chunk] = lax.optimization_barrier((half, parts[chunk]))
        pieces = send_chunk(parts[chunk], inp_at, tm_at, inp_size, tm_size)
        if chunk:
            lhs, rhs = finish_chunk(half, pol_size, cols)
            out = correlate(lhs, rhs, out, (chunk - 1) * per_chunk, own_channels)
            out, pieces = lax.optimization_barrier((out, pieces))
        half = assemble_chunk(pieces, inp_at, inp_size, tm_size, cols)
    lhs, rhs = finish_chunk(half, pol_size, cols)
    return correlate(lhs, rhs, out, (chunks - 1) * per_chunk, own_channels)


def correlate_kernel(scale, lhs_ref, rhs_ref, *rest):
    out_ref = rest[-1]
    rows = out_ref.shape[2]
    for k in range(lhs_ref.shape[0]):
        acc = jnp.dot(lhs_ref[k], rhs_ref[k], preferred_element_type=jnp.float32) * scale
        out_ref[k, 0] = acc[:rows]
        out_ref[k, 1] = acc[rows:]


def correlate(lhs, rhs, prev, first_channel, own_channels):
    count, two_rows, depth = lhs.shape
    cols = rhs.shape[2]
    rows = two_rows // 2
    step = 2 if count % 2 == 0 else 1
    offset = first_channel // step
    in_specs = [
        pl.BlockSpec((step, two_rows, depth), lambda c: (c, 0, 0)),
        pl.BlockSpec((step, depth, cols), lambda c: (c, 0, 0)),
    ]
    args = [lhs, rhs]
    aliases = {}
    if prev is not None:
        in_specs.append(pl.BlockSpec(memory_space=pl.ANY))
        args.append(prev)
        aliases = {2: 0}
    flops = 2 * count * two_rows * depth * cols
    out_bytes = count * two_rows * cols * 4
    return pl.pallas_call(
        functools.partial(correlate_kernel, 1.0 / (depth // 2)),
        grid=(count // step,),
        in_specs=in_specs,
        out_specs=pl.BlockSpec((step, 2, rows, cols), lambda c: (c + offset, 0, 0, 0)),
        out_shape=jax.ShapeDtypeStruct((own_channels, 2, rows, cols), jnp.float32),
        input_output_aliases=aliases,
        cost_estimate=pl.CostEstimate(
            flops=flops, bytes_accessed=out_bytes + lhs.size * 2 + rhs.size * 2, transcendentals=0
        ),
    )(*args)


def send_chunk(blocks, inp_at, tm_at, inp_size, tm_size):
    group_size = blocks.shape[0]
    pieces = []
    for inp_step in range(inp_size):
        for tm_step in range(tm_size):
            target = ((inp_at + inp_step) % inp_size) * tm_size + (tm_at + tm_step) % tm_size
            block = lax.dynamic_index_in_dim(blocks, target, 0, keepdims=False)
            if inp_step or tm_step:
                route = [
                    (g, ((g // tm_size + inp_step) % inp_size) * tm_size + (g % tm_size + tm_step) % tm_size)
                    for g in range(group_size)
                ]
                block = lax.ppermute(block, ("inp", "tm"), route)
            pieces.append(block)
    return pieces


def assemble_chunk(pieces, inp_at, inp_size, tm_size, cols):
    own_channels, _, spectra_here, inputs_here = pieces[0].shape
    half = jnp.zeros((own_channels, 2, tm_size, spectra_here, cols), jnp.bfloat16)
    for inp_step in range(inp_size):
        for tm_step in range(tm_size):
            block = pieces[inp_step * tm_size + tm_step]
            source_inp = (inp_at + inp_size - inp_step) % inp_size
            half = lax.dynamic_update_slice(
                half, block[:, :, None], (0, 0, tm_step, 0, source_inp * inputs_here)
            )
    return half


def finish_chunk(half, pol_size, cols):
    own_channels, _, tm_size, spectra_here, _ = half.shape
    if pol_size == 2:
        partner = lax.ppermute(half, "pol", [(0, 1), (1, 0)])
        both = jnp.stack([half, partner], axis=1)
    else:
        both = lax.all_gather(half, "pol", axis=1, tiled=False)
    depth = pol_size * 2 * tm_size * spectra_here
    left_all = both.reshape(own_channels, depth, cols)
    rows_here = cols // pol_size
    row_start = lax.axis_index("pol") * rows_here
    own_rows = lax.dynamic_slice_in_dim(both, row_start, rows_here, 5)
    swapped = jnp.stack([own_rows[:, :, 1], -own_rows[:, :, 0]], axis=2)
    lhs = jnp.stack([own_rows, swapped], axis=1).reshape(own_channels, 2, depth, rows_here)
    lhs = lhs.transpose(0, 1, 3, 2).reshape(own_channels, 2 * rows_here, depth)
    return lhs, left_all


def solution(mesh):
    return jax.shard_map(
        per_device,
        mesh=mesh,
        in_specs=(P(("group", "inp"), ("tm", "pol")),),
        out_specs=P(("group", "inp", "tm"), None, "pol", None),
        check_vma=False,
    )
```

```python
import functools
import math

import jax
import jax.numpy as jnp
from jax import lax
from jax.experimental import pallas as pl
from jax.sharding import PartitionSpec as P

CH = 512
TAPS = 16


def shifted(block, axis, distance):
    devices = range(lax.axis_size(axis))
    route = [(i - distance, i) for i in devices if i - distance in devices]
    return lax.ppermute(block, axis, route)


def prototype(tap_count, frame_len):
    length = tap_count * frame_len
    sample = lax.broadcasted_iota(jnp.int32, (length,), 0).astype(jnp.float32)
    centred = (sample - (length - 1) / 2.0) / frame_len
    window = 0.5 - 0.5 * jnp.cos(2.0 * math.pi * (sample + 0.5) / length)
    angle = math.pi * centred
    filter_taps = jnp.sin(angle) / angle * window
    filter_taps = filter_taps / jnp.sqrt(jnp.sum(filter_taps * filter_taps))
    return filter_taps.reshape(tap_count, frame_len)


def dft_table_t(frame_len):
    channel_idx = lax.broadcasted_iota(jnp.int32, (frame_len // 2, frame_len), 0)
    sample_idx = lax.broadcasted_iota(jnp.int32, (frame_len // 2, frame_len), 1)
    phase = (sample_idx * channel_idx % frame_len).astype(jnp.float32) * (2.0 * math.pi / frame_len)
    table = jnp.stack([jnp.cos(phase), -jnp.sin(phase)], axis=1)
    return table.reshape(frame_len, frame_len).astype(jnp.bfloat16)


def filter_kernel(taps_ref, own_ref, history_ref, out_ref):
    spectra_here, inputs_here, frame_len = out_ref.shape
    tile_rows, tile_cols = 16, 128
    col_tiles = frame_len // tile_cols

    def body(tile, carry):
        r0 = pl.multiple_of((tile // col_tiles) * tile_rows, tile_rows)
        c0 = pl.multiple_of((tile % col_tiles) * tile_cols, tile_cols)
        taps = [taps_ref[k : k + 1, pl.ds(c0, tile_cols)] for k in range(TAPS)]
        sums = [None] * spectra_here
        for j in range(spectra_here + TAPS - 1):
            if j < TAPS - 1:
                col = (spectra_here - (TAPS - 1) + j) * frame_len
                block = history_ref[pl.ds(r0, tile_rows), pl.ds(col + c0, tile_cols)]
            else:
                col = (j - (TAPS - 1)) * frame_len
                block = own_ref[pl.ds(r0, tile_rows), pl.ds(col + c0, tile_cols)]
            block = block.astype(jnp.float32)
            for s in range(max(0, j - (TAPS - 1)), min(spectra_here - 1, j) + 1):
                term = taps[j - s] * block
                sums[s] = term if sums[s] is None else sums[s] + term
        for s in range(spectra_here):
            out_ref[s, pl.ds(r0, tile_rows), pl.ds(c0, tile_cols)] = sums[s].astype(out_ref.dtype)
        return carry

    lax.fori_loop(0, (inputs_here // tile_rows) * col_tiles, body, 0)


def polyphase_filter(filter_taps, own, history, frame_len):
    inputs_here = own.shape[0]
    spectra_here = own.shape[1] // frame_len
    rows = 32 if inputs_here % 32 == 0 else inputs_here
    return pl.pallas_call(
        filter_kernel,
        grid=(inputs_here // rows,),
        in_specs=[
            pl.BlockSpec((TAPS, frame_len), lambda r: (0, 0)),
            pl.BlockSpec((rows, spectra_here * frame_len), lambda r: (r, 0)),
            pl.BlockSpec((rows, spectra_here * frame_len), lambda r: (r, 0)),
        ],
        out_specs=pl.BlockSpec((spectra_here, rows, frame_len), lambda r: (0, r, 0)),
        out_shape=jax.ShapeDtypeStruct((spectra_here, inputs_here, frame_len), jnp.bfloat16),
        cost_estimate=pl.CostEstimate(
            flops=2 * TAPS * own.size, bytes_accessed=3 * own.size * 2, transcendentals=0
        ),
    )(filter_taps, own, history)


def per_device(voltages):
    inputs_here = voltages.shape[0]
    frame_len = 2 * CH
    spectra_here = voltages.shape[1] // frame_len
    history = shifted(voltages, ("tm", "pol"), 1)
    filtered = polyphase_filter(prototype(TAPS, frame_len), voltages, history, frame_len)
    spectra = lax.dot_general(
        dft_table_t(frame_len),
        filtered.reshape(spectra_here * inputs_here, frame_len),
        (((1,), (1,)), ((), ())),
        preferred_element_type=jnp.float32,
    )
    spectra = spectra.astype(jnp.bfloat16).reshape(CH, 2, spectra_here, inputs_here)
    inp_size = lax.axis_size("inp")
    tm_size = lax.axis_size("tm")
    pol_size = lax.axis_size("pol")
    group_size = inp_size * tm_size
    own_channels = CH // group_size
    blocks = spectra.reshape(group_size, own_channels, 2, spectra_here, inputs_here)
    inp_at = lax.axis_index("inp")
    tm_at = lax.axis_index("tm")
    cols = inp_size * inputs_here
    chunks = 8 if own_channels % 16 == 0 else 1
    per_chunk = own_channels // chunks
    parts = [blocks[:, chunk * per_chunk : (chunk + 1) * per_chunk] for chunk in range(chunks)]
    out = None
    half = None
    for chunk in range(chunks):
        if chunk:
            half, parts[chunk] = lax.optimization_barrier((half, parts[chunk]))
        pieces = send_chunk(parts[chunk], inp_at, tm_at, inp_size, tm_size)
        if chunk:
            lhs, rhs = finish_chunk(half, pol_size, cols)
            out = correlate(lhs, rhs, out, (chunk - 1) * per_chunk, own_channels)
            out, pieces = lax.optimization_barrier((out, pieces))
        half = assemble_chunk(pieces, inp_at, inp_size, tm_size, cols)
    lhs, rhs = finish_chunk(half, pol_size, cols)
    return correlate(lhs, rhs, out, (chunks - 1) * per_chunk, own_channels)


def correlate_kernel(scale, lhs_ref, rhs_ref, *rest):
    out_ref = rest[-1]
    rows = out_ref.shape[2]
    for k in range(lhs_ref.shape[0]):
        acc = jnp.dot(lhs_ref[k], rhs_ref[k], preferred_element_type=jnp.float32) * scale
        out_ref[k, 0] = acc[:rows]
        out_ref[k, 1] = acc[rows:]


def correlate(lhs, rhs, prev, first_channel, own_channels):
    count, two_rows, depth = lhs.shape
    cols = rhs.shape[2]
    rows = two_rows // 2
    step = 2 if count % 2 == 0 else 1
    offset = first_channel // step
    in_specs = [
        pl.BlockSpec((step, two_rows, depth), lambda c: (c, 0, 0)),
        pl.BlockSpec((step, depth, cols), lambda c: (c, 0, 0)),
    ]
    args = [lhs, rhs]
    aliases = {}
    if prev is not None:
        in_specs.append(pl.BlockSpec(memory_space=pl.ANY))
        args.append(prev)
        aliases = {2: 0}
    flops = 2 * count * two_rows * depth * cols
    out_bytes = count * two_rows * cols * 4
    return pl.pallas_call(
        functools.partial(correlate_kernel, 1.0 / (depth // 2)),
        grid=(count // step,),
        in_specs=in_specs,
        out_specs=pl.BlockSpec((step, 2, rows, cols), lambda c: (c + offset, 0, 0, 0)),
        out_shape=jax.ShapeDtypeStruct((own_channels, 2, rows, cols), jnp.float32),
        input_output_aliases=aliases,
        cost_estimate=pl.CostEstimate(
            flops=flops, bytes_accessed=out_bytes + lhs.size * 2 + rhs.size * 2, transcendentals=0
        ),
    )(*args)


def send_chunk(blocks, inp_at, tm_at, inp_size, tm_size):
    group_size = blocks.shape[0]
    pieces = []
    for inp_step in range(inp_size):
        for tm_step in range(tm_size):
            target = ((inp_at + inp_step) % inp_size) * tm_size + (tm_at + tm_step) % tm_size
            block = lax.dynamic_index_in_dim(blocks, target, 0, keepdims=False)
            if inp_step or tm_step:
                route = [
                    (g, ((g // tm_size + inp_step) % inp_size) * tm_size + (g % tm_size + tm_step) % tm_size)
                    for g in range(group_size)
                ]
                block = lax.ppermute(block, ("inp", "tm"), route)
            pieces.append(block)
    return pieces


def assemble_chunk(pieces, inp_at, inp_size, tm_size, cols):
    own_channels, _, spectra_here, inputs_here = pieces[0].shape
    half = jnp.zeros((own_channels, 2, tm_size, spectra_here, cols), jnp.bfloat16)
    for inp_step in range(inp_size):
        for tm_step in range(tm_size):
            block = pieces[inp_step * tm_size + tm_step]
            source_inp = (inp_at + inp_size - inp_step) % inp_size
            half = lax.dynamic_update_slice(
                half, block[:, :, None], (0, 0, tm_step, 0, source_inp * inputs_here)
            )
    return half


def finish_chunk(half, pol_size, cols):
    own_channels, _, tm_size, spectra_here, _ = half.shape
    if pol_size == 2:
        partner = lax.ppermute(half, "pol", [(0, 1), (1, 0)])
        both = jnp.stack([half, partner], axis=1)
    else:
        both = lax.all_gather(half, "pol", axis=1, tiled=False)
    depth = pol_size * 2 * tm_size * spectra_here
    left_all = both.reshape(own_channels, depth, cols)
    rows_here = cols // pol_size
    row_start = lax.axis_index("pol") * rows_here
    own_rows = lax.dynamic_slice_in_dim(both, row_start, rows_here, 5)
    swapped = jnp.stack([own_rows[:, :, 1], -own_rows[:, :, 0]], axis=2)
    lhs = jnp.stack([own_rows, swapped], axis=1).reshape(own_channels, 2, depth, rows_here)
    lhs = lhs.transpose(0, 1, 3, 2).reshape(own_channels, 2 * rows_here, depth)
    return lhs, left_all


def solution(mesh):
    return jax.shard_map(
        per_device,
        mesh=mesh,
        in_specs=(P(("group", "inp"), ("tm", "pol")),),
        out_specs=P(("group", "inp", "tm"), None, "pol", None),
        check_vma=False,
    )
```

```python
import functools
import math

import jax
import jax.numpy as jnp
from jax import lax
from jax.experimental import pallas as pl
from jax.sharding import PartitionSpec as P

CH = 512
TAPS = 16


def shifted(block, axis, distance):
    devices = range(lax.axis_size(axis))
    route = [(i - distance, i) for i in devices if i - distance in devices]
    return lax.ppermute(block, axis, route)


def prototype(tap_count, frame_len):
    length = tap_count * frame_len
    sample = lax.broadcasted_iota(jnp.int32, (length,), 0).astype(jnp.float32)
    centred = (sample - (length - 1) / 2.0) / frame_len
    window = 0.5 - 0.5 * jnp.cos(2.0 * math.pi * (sample + 0.5) / length)
    angle = math.pi * centred
    filter_taps = jnp.sin(angle) / angle * window
    filter_taps = filter_taps / jnp.sqrt(jnp.sum(filter_taps * filter_taps))
    return filter_taps.reshape(tap_count, frame_len)


def dft_table_t(frame_len):
    channel_idx = lax.broadcasted_iota(jnp.int32, (frame_len // 2, frame_len), 0)
    sample_idx = lax.broadcasted_iota(jnp.int32, (frame_len // 2, frame_len), 1)
    phase = (sample_idx * channel_idx % frame_len).astype(jnp.float32) * (2.0 * math.pi / frame_len)
    table = jnp.stack([jnp.cos(phase), -jnp.sin(phase)], axis=1)
    return table.reshape(frame_len, frame_len).astype(jnp.bfloat16)


def filter_kernel(taps_ref, own_ref, history_ref, out_ref):
    spectra_here, inputs_here, frame_len = out_ref.shape
    tile_rows, tile_cols = 16, 128
    col_tiles = frame_len // tile_cols

    def body(tile, carry):
        r0 = pl.multiple_of((tile // col_tiles) * tile_rows, tile_rows)
        c0 = pl.multiple_of((tile % col_tiles) * tile_cols, tile_cols)
        taps = [taps_ref[k : k + 1, pl.ds(c0, tile_cols)] for k in range(TAPS)]
        sums = [None] * spectra_here
        for j in range(spectra_here + TAPS - 1):
            if j < TAPS - 1:
                col = (spectra_here - (TAPS - 1) + j) * frame_len
                block = history_ref[pl.ds(r0, tile_rows), pl.ds(col + c0, tile_cols)]
            else:
                col = (j - (TAPS - 1)) * frame_len
                block = own_ref[pl.ds(r0, tile_rows), pl.ds(col + c0, tile_cols)]
            block = block.astype(jnp.float32)
            for s in range(max(0, j - (TAPS - 1)), min(spectra_here - 1, j) + 1):
                term = taps[j - s] * block
                sums[s] = term if sums[s] is None else sums[s] + term
        for s in range(spectra_here):
            out_ref[s, pl.ds(r0, tile_rows), pl.ds(c0, tile_cols)] = sums[s].astype(out_ref.dtype)
        return carry

    lax.fori_loop(0, (inputs_here // tile_rows) * col_tiles, body, 0)


def polyphase_filter(filter_taps, own, history, frame_len):
    inputs_here = own.shape[0]
    spectra_here = own.shape[1] // frame_len
    rows = 32 if inputs_here % 32 == 0 else inputs_here
    return pl.pallas_call(
        filter_kernel,
        grid=(inputs_here // rows,),
        in_specs=[
            pl.BlockSpec((TAPS, frame_len), lambda r: (0, 0)),
            pl.BlockSpec((rows, spectra_here * frame_len), lambda r: (r, 0)),
            pl.BlockSpec((rows, spectra_here * frame_len), lambda r: (r, 0)),
        ],
        out_specs=pl.BlockSpec((spectra_here, rows, frame_len), lambda r: (0, r, 0)),
        out_shape=jax.ShapeDtypeStruct((spectra_here, inputs_here, frame_len), jnp.bfloat16),
        cost_estimate=pl.CostEstimate(
            flops=2 * TAPS * own.size, bytes_accessed=3 * own.size * 2, transcendentals=0
        ),
    )(filter_taps, own, history)


def per_device(voltages):
    inputs_here = voltages.shape[0]
    frame_len = 2 * CH
    spectra_here = voltages.shape[1] // frame_len
    history = shifted(voltages, ("tm", "pol"), 1)
    filtered = polyphase_filter(prototype(TAPS, frame_len), voltages, history, frame_len)
    spectra = lax.dot_general(
        dft_table_t(frame_len),
        filtered.reshape(spectra_here * inputs_here, frame_len),
        (((1,), (1,)), ((), ())),
        preferred_element_type=jnp.float32,
    )
    spectra = spectra.astype(jnp.bfloat16).reshape(CH, 2, spectra_here, inputs_here)
    inp_size = lax.axis_size("inp")
    tm_size = lax.axis_size("tm")
    pol_size = lax.axis_size("pol")
    group_size = inp_size * tm_size
    own_channels = CH // group_size
    blocks = spectra.reshape(group_size, own_channels, 2, spectra_here, inputs_here)
    inp_at = lax.axis_index("inp")
    tm_at = lax.axis_index("tm")
    cols = inp_size * inputs_here
    chunks = 4 if own_channels % 8 == 0 else 1
    per_chunk = own_channels // chunks
    parts = [blocks[:, chunk * per_chunk : (chunk + 1) * per_chunk] for chunk in range(chunks)]
    out = None
    half = None
    for chunk in range(chunks):
        if chunk:
            half, parts[chunk] = lax.optimization_barrier((half, parts[chunk]))
        pieces = send_chunk(parts[chunk], inp_at, tm_at, inp_size, tm_size)
        if chunk:
            lhs, rhs = finish_chunk(half, pol_size, cols)
            out = correlate(lhs, rhs, out, (chunk - 1) * per_chunk, own_channels)
            out, pieces = lax.optimization_barrier((out, pieces))
        half = assemble_chunk(pieces, inp_at, inp_size, tm_size, cols)
    lhs, rhs = finish_chunk(half, pol_size, cols)
    return correlate(lhs, rhs, out, (chunks - 1) * per_chunk, own_channels)


def correlate_kernel(scale, lhs_ref, rhs_ref, *rest):
    out_ref = rest[-1]
    rows = out_ref.shape[2]
    for k in range(lhs_ref.shape[0]):
        acc = jnp.dot(lhs_ref[k], rhs_ref[k], preferred_element_type=jnp.float32) * scale
        out_ref[k, 0] = acc[:rows]
        out_ref[k, 1] = acc[rows:]


def correlate(lhs, rhs, prev, first_channel, own_channels):
    count, two_rows, depth = lhs.shape
    cols = rhs.shape[2]
    rows = two_rows // 2
    step = 4 if count % 4 == 0 else (2 if count % 2 == 0 else 1)
    offset = first_channel // step
    in_specs = [
        pl.BlockSpec((step, two_rows, depth), lambda c: (c, 0, 0)),
        pl.BlockSpec((step, depth, cols), lambda c: (c, 0, 0)),
    ]
    args = [lhs, rhs]
    aliases = {}
    if prev is not None:
        in_specs.append(pl.BlockSpec(memory_space=pl.ANY))
        args.append(prev)
        aliases = {2: 0}
    flops = 2 * count * two_rows * depth * cols
    out_bytes = count * two_rows * cols * 4
    return pl.pallas_call(
        functools.partial(correlate_kernel, 1.0 / (depth // 2)),
        grid=(count // step,),
        in_specs=in_specs,
        out_specs=pl.BlockSpec((step, 2, rows, cols), lambda c: (c + offset, 0, 0, 0)),
        out_shape=jax.ShapeDtypeStruct((own_channels, 2, rows, cols), jnp.float32),
        input_output_aliases=aliases,
        cost_estimate=pl.CostEstimate(
            flops=flops, bytes_accessed=out_bytes + lhs.size * 2 + rhs.size * 2, transcendentals=0
        ),
    )(*args)


def send_chunk(blocks, inp_at, tm_at, inp_size, tm_size):
    group_size = blocks.shape[0]
    pieces = []
    for inp_step in range(inp_size):
        for tm_step in range(tm_size):
            target = ((inp_at + inp_step) % inp_size) * tm_size + (tm_at + tm_step) % tm_size
            block = lax.dynamic_index_in_dim(blocks, target, 0, keepdims=False)
            if inp_step or tm_step:
                route = [
                    (g, ((g // tm_size + inp_step) % inp_size) * tm_size + (g % tm_size + tm_step) % tm_size)
                    for g in range(group_size)
                ]
                block = lax.ppermute(block, ("inp", "tm"), route)
            pieces.append(block)
    return pieces


def assemble_chunk(pieces, inp_at, inp_size, tm_size, cols):
    own_channels, _, spectra_here, inputs_here = pieces[0].shape
    half = jnp.zeros((own_channels, 2, tm_size, spectra_here, cols), jnp.bfloat16)
    for inp_step in range(inp_size):
        for tm_step in range(tm_size):
            block = pieces[inp_step * tm_size + tm_step]
            source_inp = (inp_at + inp_size - inp_step) % inp_size
            half = lax.dynamic_update_slice(
                half, block[:, :, None], (0, 0, tm_step, 0, source_inp * inputs_here)
            )
    return half


def finish_chunk(half, pol_size, cols):
    own_channels, _, tm_size, spectra_here, _ = half.shape
    if pol_size == 2:
        partner = lax.ppermute(half, "pol", [(0, 1), (1, 0)])
        both = jnp.stack([half, partner], axis=1)
    else:
        both = lax.all_gather(half, "pol", axis=1, tiled=False)
    depth = pol_size * 2 * tm_size * spectra_here
    left_all = both.reshape(own_channels, depth, cols)
    rows_here = cols // pol_size
    row_start = lax.axis_index("pol") * rows_here
    own_rows = lax.dynamic_slice_in_dim(both, row_start, rows_here, 5)
    swapped = jnp.stack([own_rows[:, :, 1], -own_rows[:, :, 0]], axis=2)
    lhs = jnp.stack([own_rows, swapped], axis=1).reshape(own_channels, 2, depth, rows_here)
    lhs = lhs.transpose(0, 1, 3, 2).reshape(own_channels, 2 * rows_here, depth)
    return lhs, left_all


def solution(mesh):
    return jax.shard_map(
        per_device,
        mesh=mesh,
        in_specs=(P(("group", "inp"), ("tm", "pol")),),
        out_specs=P(("group", "inp", "tm"), None, "pol", None),
        check_vma=False,
    )
```

```python
import functools
import math

import jax
import jax.numpy as jnp
from jax import lax
from jax.experimental import pallas as pl
from jax.sharding import PartitionSpec as P

CH = 512
TAPS = 16


def shifted(block, axis, distance):
    devices = range(lax.axis_size(axis))
    route = [(i - distance, i) for i in devices if i - distance in devices]
    return lax.ppermute(block, axis, route)


def prototype(tap_count, frame_len):
    length = tap_count * frame_len
    sample = lax.broadcasted_iota(jnp.int32, (length,), 0).astype(jnp.float32)
    centred = (sample - (length - 1) / 2.0) / frame_len
    window = 0.5 - 0.5 * jnp.cos(2.0 * math.pi * (sample + 0.5) / length)
    angle = math.pi * centred
    filter_taps = jnp.sin(angle) / angle * window
    filter_taps = filter_taps / jnp.sqrt(jnp.sum(filter_taps * filter_taps))
    return filter_taps.reshape(tap_count, frame_len)


def dft_table_t(frame_len):
    channel_idx = lax.broadcasted_iota(jnp.int32, (frame_len // 2, frame_len), 0)
    sample_idx = lax.broadcasted_iota(jnp.int32, (frame_len // 2, frame_len), 1)
    phase = (sample_idx * channel_idx % frame_len).astype(jnp.float32) * (2.0 * math.pi / frame_len)
    table = jnp.stack([jnp.cos(phase), -jnp.sin(phase)], axis=1)
    return table.reshape(frame_len, frame_len).astype(jnp.bfloat16)


def filter_kernel(taps_ref, own_ref, history_ref, out_ref):
    spectra_here, inputs_here, frame_len = out_ref.shape
    tile_rows, tile_cols = 16, 128
    col_tiles = frame_len // tile_cols

    def body(tile, carry):
        r0 = pl.multiple_of((tile // col_tiles) * tile_rows, tile_rows)
        c0 = pl.multiple_of((tile % col_tiles) * tile_cols, tile_cols)
        taps = [taps_ref[k : k + 1, pl.ds(c0, tile_cols)] for k in range(TAPS)]
        sums = [None] * spectra_here
        for j in range(spectra_here + TAPS - 1):
            if j < TAPS - 1:
                col = (spectra_here - (TAPS - 1) + j) * frame_len
                block = history_ref[pl.ds(r0, tile_rows), pl.ds(col + c0, tile_cols)]
            else:
                col = (j - (TAPS - 1)) * frame_len
                block = own_ref[pl.ds(r0, tile_rows), pl.ds(col + c0, tile_cols)]
            block = block.astype(jnp.float32)
            for s in range(max(0, j - (TAPS - 1)), min(spectra_here - 1, j) + 1):
                term = taps[j - s] * block
                sums[s] = term if sums[s] is None else sums[s] + term
        for s in range(spectra_here):
            out_ref[s, pl.ds(r0, tile_rows), pl.ds(c0, tile_cols)] = sums[s].astype(out_ref.dtype)
        return carry

    lax.fori_loop(0, (inputs_here // tile_rows) * col_tiles, body, 0)


def polyphase_filter(filter_taps, own, history, frame_len):
    inputs_here = own.shape[0]
    spectra_here = own.shape[1] // frame_len
    rows = 32 if inputs_here % 32 == 0 else inputs_here
    return pl.pallas_call(
        filter_kernel,
        grid=(inputs_here // rows,),
        in_specs=[
            pl.BlockSpec((TAPS, frame_len), lambda r: (0, 0)),
            pl.BlockSpec((rows, spectra_here * frame_len), lambda r: (r, 0)),
            pl.BlockSpec((rows, spectra_here * frame_len), lambda r: (r, 0)),
        ],
        out_specs=pl.BlockSpec((spectra_here, rows, frame_len), lambda r: (0, r, 0)),
        out_shape=jax.ShapeDtypeStruct((spectra_here, inputs_here, frame_len), jnp.bfloat16),
        cost_estimate=pl.CostEstimate(
            flops=2 * TAPS * own.size, bytes_accessed=3 * own.size * 2, transcendentals=0
        ),
    )(filter_taps, own, history)


def per_device(voltages):
    inputs_here = voltages.shape[0]
    frame_len = 2 * CH
    spectra_here = voltages.shape[1] // frame_len
    history = shifted(voltages, ("tm", "pol"), 1)
    filtered = polyphase_filter(prototype(TAPS, frame_len), voltages, history, frame_len)
    spectra = lax.dot_general(
        dft_table_t(frame_len),
        filtered.reshape(spectra_here * inputs_here, frame_len),
        (((1,), (1,)), ((), ())),
        preferred_element_type=jnp.float32,
    )
    spectra = spectra.astype(jnp.bfloat16).reshape(CH, 2, spectra_here, inputs_here)
    inp_size = lax.axis_size("inp")
    tm_size = lax.axis_size("tm")
    pol_size = lax.axis_size("pol")
    group_size = inp_size * tm_size
    own_channels = CH // group_size
    blocks = spectra.reshape(group_size, own_channels, 2, spectra_here, inputs_here)
    inp_at = lax.axis_index("inp")
    tm_at = lax.axis_index("tm")
    cols = inp_size * inputs_here
    chunks = 4 if own_channels % 8 == 0 else 1
    per_chunk = own_channels // chunks
    parts = [blocks[:, chunk * per_chunk : (chunk + 1) * per_chunk] for chunk in range(chunks)]
    out = None
    half = None
    for chunk in range(chunks):
        if chunk:
            half, parts[chunk] = lax.optimization_barrier((half, parts[chunk]))
        pieces = send_chunk(parts[chunk], inp_at, tm_at, inp_size, tm_size)
        if chunk:
            lhs, rhs = finish_chunk(half, pol_size, cols)
            out = correlate(lhs, rhs, out, (chunk - 1) * per_chunk, own_channels)
            out, pieces = lax.optimization_barrier((out, pieces))
        half = assemble_chunk(pieces, inp_at, inp_size, tm_size, cols)
    lhs, rhs = finish_chunk(half, pol_size, cols)
    return correlate(lhs, rhs, out, (chunks - 1) * per_chunk, own_channels)


def correlate_kernel(scale, lhs_ref, rhs_ref, *rest):
    out_ref = rest[-1]
    rows = out_ref.shape[2]
    for k in range(lhs_ref.shape[0]):
        acc = lax.dot_general(
            lhs_ref[k], rhs_ref[k], (((0,), (0,)), ((), ())), preferred_element_type=jnp.float32
        ) * scale
        out_ref[k, 0] = acc[:rows]
        out_ref[k, 1] = acc[rows:]


def correlate(lhs, rhs, prev, first_channel, own_channels):
    count, depth, two_rows = lhs.shape
    cols = rhs.shape[2]
    rows = two_rows // 2
    step = 4 if count % 4 == 0 else (2 if count % 2 == 0 else 1)
    offset = first_channel // step
    in_specs = [
        pl.BlockSpec((step, depth, two_rows), lambda c: (c, 0, 0)),
        pl.BlockSpec((step, depth, cols), lambda c: (c, 0, 0)),
    ]
    args = [lhs, rhs]
    aliases = {}
    if prev is not None:
        in_specs.append(pl.BlockSpec(memory_space=pl.ANY))
        args.append(prev)
        aliases = {2: 0}
    flops = 2 * count * two_rows * depth * cols
    out_bytes = count * two_rows * cols * 4
    return pl.pallas_call(
        functools.partial(correlate_kernel, 1.0 / (depth // 2)),
        grid=(count // step,),
        in_specs=in_specs,
        out_specs=pl.BlockSpec((step, 2, rows, cols), lambda c: (c + offset, 0, 0, 0)),
        out_shape=jax.ShapeDtypeStruct((own_channels, 2, rows, cols), jnp.float32),
        input_output_aliases=aliases,
        cost_estimate=pl.CostEstimate(
            flops=flops, bytes_accessed=out_bytes + lhs.size * 2 + rhs.size * 2, transcendentals=0
        ),
    )(*args)


def send_chunk(blocks, inp_at, tm_at, inp_size, tm_size):
    group_size = blocks.shape[0]
    pieces = []
    for inp_step in range(inp_size):
        for tm_step in range(tm_size):
            target = ((inp_at + inp_step) % inp_size) * tm_size + (tm_at + tm_step) % tm_size
            block = lax.dynamic_index_in_dim(blocks, target, 0, keepdims=False)
            if inp_step or tm_step:
                route = [
                    (g, ((g // tm_size + inp_step) % inp_size) * tm_size + (g % tm_size + tm_step) % tm_size)
                    for g in range(group_size)
                ]
                block = lax.ppermute(block, ("inp", "tm"), route)
            pieces.append(block)
    return pieces


def assemble_chunk(pieces, inp_at, inp_size, tm_size, cols):
    own_channels, _, spectra_here, inputs_here = pieces[0].shape
    half = jnp.zeros((own_channels, 2, tm_size, spectra_here, cols), jnp.bfloat16)
    for inp_step in range(inp_size):
        for tm_step in range(tm_size):
            block = pieces[inp_step * tm_size + tm_step]
            source_inp = (inp_at + inp_size - inp_step) % inp_size
            half = lax.dynamic_update_slice(
                half, block[:, :, None], (0, 0, tm_step, 0, source_inp * inputs_here)
            )
    return half


def finish_chunk(half, pol_size, cols):
    own_channels, _, tm_size, spectra_here, _ = half.shape
    if pol_size == 2:
        partner = lax.ppermute(half, "pol", [(0, 1), (1, 0)])
        both = jnp.stack([half, partner], axis=1)
    else:
        both = lax.all_gather(half, "pol", axis=1, tiled=False)
    depth = pol_size * 2 * tm_size * spectra_here
    left_all = both.reshape(own_channels, depth, cols)
    rows_here = cols // pol_size
    row_start = lax.axis_index("pol") * rows_here
    own_rows = lax.dynamic_slice_in_dim(both, row_start, rows_here, 5)
    swapped = jnp.stack([own_rows[:, :, 1], -own_rows[:, :, 0]], axis=2)
    lhs = jnp.concatenate([own_rows, swapped], axis=5).reshape(own_channels, depth, 2 * rows_here)
    return lhs, left_all


def solution(mesh):
    return jax.shard_map(
        per_device,
        mesh=mesh,
        in_specs=(P(("group", "inp"), ("tm", "pol")),),
        out_specs=P(("group", "inp", "tm"), None, "pol", None),
        check_vma=False,
    )
```

```python
import functools
import math

import jax
import jax.numpy as jnp
from jax import lax
from jax.experimental import pallas as pl
from jax.sharding import PartitionSpec as P

CH = 512
TAPS = 16


def shifted(block, axis, distance):
    devices = range(lax.axis_size(axis))
    route = [(i - distance, i) for i in devices if i - distance in devices]
    return lax.ppermute(block, axis, route)


def prototype(tap_count, frame_len):
    length = tap_count * frame_len
    sample = lax.broadcasted_iota(jnp.int32, (length,), 0).astype(jnp.float32)
    centred = (sample - (length - 1) / 2.0) / frame_len
    window = 0.5 - 0.5 * jnp.cos(2.0 * math.pi * (sample + 0.5) / length)
    angle = math.pi * centred
    filter_taps = jnp.sin(angle) / angle * window
    filter_taps = filter_taps / jnp.sqrt(jnp.sum(filter_taps * filter_taps))
    return filter_taps.reshape(tap_count, frame_len)


def dft_table_t(frame_len):
    channel_idx = lax.broadcasted_iota(jnp.int32, (frame_len // 2, frame_len), 0)
    sample_idx = lax.broadcasted_iota(jnp.int32, (frame_len // 2, frame_len), 1)
    phase = (sample_idx * channel_idx % frame_len).astype(jnp.float32) * (2.0 * math.pi / frame_len)
    table = jnp.stack([jnp.cos(phase), -jnp.sin(phase)], axis=1)
    return table.reshape(frame_len, frame_len).astype(jnp.bfloat16)


def filter_kernel(taps_ref, own_ref, history_ref, out_ref):
    spectra_here, inputs_here, frame_len = out_ref.shape
    tile_rows, tile_cols = 16, 128
    col_tiles = frame_len // tile_cols

    def body(tile, carry):
        r0 = pl.multiple_of((tile // col_tiles) * tile_rows, tile_rows)
        c0 = pl.multiple_of((tile % col_tiles) * tile_cols, tile_cols)
        taps = [taps_ref[k : k + 1, pl.ds(c0, tile_cols)] for k in range(TAPS)]
        sums = [None] * spectra_here
        for j in range(spectra_here + TAPS - 1):
            if j < TAPS - 1:
                col = (spectra_here - (TAPS - 1) + j) * frame_len
                block = history_ref[pl.ds(r0, tile_rows), pl.ds(col + c0, tile_cols)]
            else:
                col = (j - (TAPS - 1)) * frame_len
                block = own_ref[pl.ds(r0, tile_rows), pl.ds(col + c0, tile_cols)]
            block = block.astype(jnp.float32)
            for s in range(max(0, j - (TAPS - 1)), min(spectra_here - 1, j) + 1):
                term = taps[j - s] * block
                sums[s] = term if sums[s] is None else sums[s] + term
        for s in range(spectra_here):
            out_ref[s, pl.ds(r0, tile_rows), pl.ds(c0, tile_cols)] = sums[s].astype(out_ref.dtype)
        return carry

    lax.fori_loop(0, (inputs_here // tile_rows) * col_tiles, body, 0)


def polyphase_filter(filter_taps, own, history, frame_len):
    inputs_here = own.shape[0]
    spectra_here = own.shape[1] // frame_len
    rows = 32 if inputs_here % 32 == 0 else inputs_here
    return pl.pallas_call(
        filter_kernel,
        grid=(inputs_here // rows,),
        in_specs=[
            pl.BlockSpec((TAPS, frame_len), lambda r: (0, 0)),
            pl.BlockSpec((rows, spectra_here * frame_len), lambda r: (r, 0)),
            pl.BlockSpec((rows, spectra_here * frame_len), lambda r: (r, 0)),
        ],
        out_specs=pl.BlockSpec((spectra_here, rows, frame_len), lambda r: (0, r, 0)),
        out_shape=jax.ShapeDtypeStruct((spectra_here, inputs_here, frame_len), jnp.bfloat16),
        cost_estimate=pl.CostEstimate(
            flops=2 * TAPS * own.size, bytes_accessed=3 * own.size * 2, transcendentals=0
        ),
    )(filter_taps, own, history)


def per_device(voltages):
    inputs_here = voltages.shape[0]
    frame_len = 2 * CH
    spectra_here = voltages.shape[1] // frame_len
    history = shifted(voltages, ("tm", "pol"), 1)
    filtered = polyphase_filter(prototype(TAPS, frame_len), voltages, history, frame_len)
    spectra = lax.dot_general(
        dft_table_t(frame_len),
        filtered.reshape(spectra_here * inputs_here, frame_len),
        (((1,), (1,)), ((), ())),
        preferred_element_type=jnp.float32,
    )
    spectra = spectra.astype(jnp.bfloat16).reshape(CH, 2, spectra_here, inputs_here)
    inp_size = lax.axis_size("inp")
    tm_size = lax.axis_size("tm")
    pol_size = lax.axis_size("pol")
    group_size = inp_size * tm_size
    own_channels = CH // group_size
    blocks = spectra.reshape(group_size, own_channels, 2, spectra_here, inputs_here)
    inp_at = lax.axis_index("inp")
    tm_at = lax.axis_index("tm")
    cols = inp_size * inputs_here
    chunks = 4 if own_channels % 8 == 0 else 1
    per_chunk = own_channels // chunks
    parts = [blocks[:, chunk * per_chunk : (chunk + 1) * per_chunk] for chunk in range(chunks)]
    out = None
    half = None
    for chunk in range(chunks):
        if chunk:
            half, parts[chunk] = lax.optimization_barrier((half, parts[chunk]))
        pieces = send_chunk(parts[chunk], inp_at, tm_at, inp_size, tm_size)
        if chunk:
            lhs, rhs = finish_chunk(half, pol_size, cols)
            out = correlate(lhs, rhs, out, (chunk - 1) * per_chunk, own_channels)
            out, pieces = lax.optimization_barrier((out, pieces))
        half = assemble_chunk(pieces, inp_at, inp_size, tm_size, cols)
    lhs, rhs = finish_chunk(half, pol_size, cols)
    return correlate(lhs, rhs, out, (chunks - 1) * per_chunk, own_channels)


def correlate_kernel(scale, lhs_ref, lhs2_ref, rhs_ref, rhs2_ref, *rest):
    out_ref = rest[-1]
    rows = out_ref.shape[2]
    for k in range(lhs_ref.shape[0]):
        acc = lax.dot_general(
            lhs_ref[k], rhs_ref[k], (((0,), (0,)), ((), ())), preferred_element_type=jnp.float32
        ) + lax.dot_general(
            lhs2_ref[k], rhs2_ref[k], (((0,), (0,)), ((), ())), preferred_element_type=jnp.float32
        )
        acc = acc * scale
        out_ref[k, 0] = acc[:rows]
        out_ref[k, 1] = acc[rows:]


def correlate(lhs, rhs, prev, first_channel, own_channels):
    count, depth, two_rows = lhs[0].shape
    cols = rhs[0].shape[2]
    rows = two_rows // 2
    step = 4 if count % 4 == 0 else (2 if count % 2 == 0 else 1)
    offset = first_channel // step
    in_specs = [pl.BlockSpec((step, depth, two_rows), lambda c: (c, 0, 0))] * 2 + [
        pl.BlockSpec((step, depth, cols), lambda c: (c, 0, 0))
    ] * 2
    args = [lhs[0], lhs[1], rhs[0], rhs[1]]
    aliases = {}
    if prev is not None:
        in_specs.append(pl.BlockSpec(memory_space=pl.ANY))
        args.append(prev)
        aliases = {4: 0}
    flops = 4 * count * two_rows * depth * cols
    out_bytes = count * two_rows * cols * 4
    return pl.pallas_call(
        functools.partial(correlate_kernel, 1.0 / depth),
        grid=(count // step,),
        in_specs=in_specs,
        out_specs=pl.BlockSpec((step, 2, rows, cols), lambda c: (c + offset, 0, 0, 0)),
        out_shape=jax.ShapeDtypeStruct((own_channels, 2, rows, cols), jnp.float32),
        input_output_aliases=aliases,
        cost_estimate=pl.CostEstimate(
            flops=flops, bytes_accessed=out_bytes + 2 * (lhs[0].size + rhs[0].size) * 2, transcendentals=0
        ),
    )(*args)


def send_chunk(blocks, inp_at, tm_at, inp_size, tm_size):
    group_size = blocks.shape[0]
    pieces = []
    for inp_step in range(inp_size):
        for tm_step in range(tm_size):
            target = ((inp_at + inp_step) % inp_size) * tm_size + (tm_at + tm_step) % tm_size
            block = lax.dynamic_index_in_dim(blocks, target, 0, keepdims=False)
            if inp_step or tm_step:
                route = [
                    (g, ((g // tm_size + inp_step) % inp_size) * tm_size + (g % tm_size + tm_step) % tm_size)
                    for g in range(group_size)
                ]
                block = lax.ppermute(block, ("inp", "tm"), route)
            pieces.append(block)
    return pieces


def assemble_chunk(pieces, inp_at, inp_size, tm_size, cols):
    own_channels, _, spectra_here, inputs_here = pieces[0].shape
    half = jnp.zeros((own_channels, 2, tm_size, spectra_here, cols), jnp.bfloat16)
    for inp_step in range(inp_size):
        for tm_step in range(tm_size):
            block = pieces[inp_step * tm_size + tm_step]
            source_inp = (inp_at + inp_size - inp_step) % inp_size
            half = lax.dynamic_update_slice(
                half, block[:, :, None], (0, 0, tm_step, 0, source_inp * inputs_here)
            )
    return half


def finish_chunk(half, pol_size, cols):
    own_channels, _, tm_size, spectra_here, _ = half.shape
    if pol_size != 2:
        raise ValueError("pol size")
    partner = lax.ppermute(half, "pol", [(0, 1), (1, 0)])
    depth = 2 * tm_size * spectra_here
    rows_here = cols // pol_size
    row_start = lax.axis_index("pol") * rows_here
    lhs, rhs = [], []
    for part in (half, partner):
        own_rows = lax.dynamic_slice_in_dim(part, row_start, rows_here, 4)
        swapped = jnp.stack([own_rows[:, 1], -own_rows[:, 0]], axis=1)
        lhs.append(jnp.concatenate([own_rows, swapped], axis=4).reshape(own_channels, depth, 2 * rows_here))
        rhs.append(part.reshape(own_channels, depth, cols))
    return lhs, rhs


def solution(mesh):
    return jax.shard_map(
        per_device,
        mesh=mesh,
        in_specs=(P(("group", "inp"), ("tm", "pol")),),
        out_specs=P(("group", "inp", "tm"), None, "pol", None),
        check_vma=False,
    )
```

```python
import functools
import math

import jax
import jax.numpy as jnp
from jax import lax
from jax.experimental import pallas as pl
from jax.sharding import PartitionSpec as P

CH = 512
TAPS = 16


def shifted(block, axis, distance):
    devices = range(lax.axis_size(axis))
    route = [(i - distance, i) for i in devices if i - distance in devices]
    return lax.ppermute(block, axis, route)


def prototype(tap_count, frame_len):
    length = tap_count * frame_len
    sample = lax.broadcasted_iota(jnp.int32, (length,), 0).astype(jnp.float32)
    centred = (sample - (length - 1) / 2.0) / frame_len
    window = 0.5 - 0.5 * jnp.cos(2.0 * math.pi * (sample + 0.5) / length)
    angle = math.pi * centred
    filter_taps = jnp.sin(angle) / angle * window
    filter_taps = filter_taps / jnp.sqrt(jnp.sum(filter_taps * filter_taps))
    return filter_taps.reshape(tap_count, frame_len)


def dft_table_t(frame_len):
    channel_idx = lax.broadcasted_iota(jnp.int32, (frame_len // 2, frame_len), 0)
    sample_idx = lax.broadcasted_iota(jnp.int32, (frame_len // 2, frame_len), 1)
    phase = (sample_idx * channel_idx % frame_len).astype(jnp.float32) * (2.0 * math.pi / frame_len)
    table = jnp.stack([jnp.cos(phase), -jnp.sin(phase)], axis=1)
    return table.reshape(frame_len, frame_len).astype(jnp.bfloat16)


def filter_kernel(taps_ref, own_ref, history_ref, out_ref):
    spectra_here, inputs_here, frame_len = out_ref.shape
    tile_rows, tile_cols = 16, 128
    col_tiles = frame_len // tile_cols

    def body(tile, carry):
        r0 = pl.multiple_of((tile // col_tiles) * tile_rows, tile_rows)
        c0 = pl.multiple_of((tile % col_tiles) * tile_cols, tile_cols)
        taps = [taps_ref[k : k + 1, pl.ds(c0, tile_cols)] for k in range(TAPS)]
        sums = [None] * spectra_here
        for j in range(spectra_here + TAPS - 1):
            if j < TAPS - 1:
                col = (spectra_here - (TAPS - 1) + j) * frame_len
                block = history_ref[pl.ds(r0, tile_rows), pl.ds(col + c0, tile_cols)]
            else:
                col = (j - (TAPS - 1)) * frame_len
                block = own_ref[pl.ds(r0, tile_rows), pl.ds(col + c0, tile_cols)]
            block = block.astype(jnp.float32)
            for s in range(max(0, j - (TAPS - 1)), min(spectra_here - 1, j) + 1):
                term = taps[j - s] * block
                sums[s] = term if sums[s] is None else sums[s] + term
        for s in range(spectra_here):
            out_ref[s, pl.ds(r0, tile_rows), pl.ds(c0, tile_cols)] = sums[s].astype(out_ref.dtype)
        return carry

    lax.fori_loop(0, (inputs_here // tile_rows) * col_tiles, body, 0)


def polyphase_filter(filter_taps, own, history, frame_len):
    inputs_here = own.shape[0]
    spectra_here = own.shape[1] // frame_len
    rows = 32 if inputs_here % 32 == 0 else inputs_here
    return pl.pallas_call(
        filter_kernel,
        grid=(inputs_here // rows,),
        in_specs=[
            pl.BlockSpec((TAPS, frame_len), lambda r: (0, 0)),
            pl.BlockSpec((rows, spectra_here * frame_len), lambda r: (r, 0)),
            pl.BlockSpec((rows, spectra_here * frame_len), lambda r: (r, 0)),
        ],
        out_specs=pl.BlockSpec((spectra_here, rows, frame_len), lambda r: (0, r, 0)),
        out_shape=jax.ShapeDtypeStruct((spectra_here, inputs_here, frame_len), jnp.bfloat16),
        cost_estimate=pl.CostEstimate(
            flops=2 * TAPS * own.size, bytes_accessed=3 * own.size * 2, transcendentals=0
        ),
    )(filter_taps, own, history)


def per_device(voltages):
    inputs_here = voltages.shape[0]
    frame_len = 2 * CH
    spectra_here = voltages.shape[1] // frame_len
    history = shifted(voltages, ("tm", "pol"), 1)
    filtered = polyphase_filter(prototype(TAPS, frame_len), voltages, history, frame_len)
    spectra = lax.dot_general(
        dft_table_t(frame_len),
        filtered.reshape(spectra_here * inputs_here, frame_len),
        (((1,), (1,)), ((), ())),
        preferred_element_type=jnp.float32,
    )
    spectra = spectra.astype(jnp.bfloat16).reshape(CH, 2, spectra_here, inputs_here)
    inp_size = lax.axis_size("inp")
    tm_size = lax.axis_size("tm")
    pol_size = lax.axis_size("pol")
    group_size = inp_size * tm_size
    own_channels = CH // group_size
    blocks = spectra.reshape(group_size, own_channels, 2, spectra_here, inputs_here)
    inp_at = lax.axis_index("inp")
    tm_at = lax.axis_index("tm")
    cols = inp_size * inputs_here
    chunks = 4 if own_channels % 8 == 0 else 1
    per_chunk = own_channels // chunks
    parts = [blocks[:, chunk * per_chunk : (chunk + 1) * per_chunk] for chunk in range(chunks)]
    out = None
    half = None
    for chunk in range(chunks):
        if chunk:
            half, parts[chunk] = lax.optimization_barrier((half, parts[chunk]))
        pieces = send_chunk(parts[chunk], inp_at, tm_at, inp_size, tm_size)
        if chunk:
            lhs, rhs = finish_chunk(half, pol_size, cols)
            out = correlate(lhs, rhs, out, (chunk - 1) * per_chunk, own_channels)
            out, pieces = lax.optimization_barrier((out, pieces))
        half = assemble_chunk(pieces, inp_at, inp_size, tm_size, cols)
    lhs, rhs = finish_chunk(half, pol_size, cols)
    return correlate(lhs, rhs, out, (chunks - 1) * per_chunk, own_channels)


def correlate_kernel(scale, lhs_ref, lhs2_ref, rhs_ref, rhs2_ref, *rest):
    out_ref = rest[-1]
    rows = out_ref.shape[2]
    for k in range(lhs_ref.shape[0]):
        acc = lax.dot_general(
            lhs_ref[k], rhs_ref[k], (((0,), (0,)), ((), ())), preferred_element_type=jnp.float32
        ) + lax.dot_general(
            lhs2_ref[k], rhs2_ref[k], (((0,), (0,)), ((), ())), preferred_element_type=jnp.float32
        )
        acc = acc * scale
        out_ref[k, 0] = acc[:rows]
        out_ref[k, 1] = acc[rows:]


def correlate(lhs, rhs, prev, first_channel, own_channels):
    count, depth, two_rows = lhs[0].shape
    cols = rhs[0].shape[2]
    rows = two_rows // 2
    step = 8 if count % 8 == 0 else (4 if count % 4 == 0 else (2 if count % 2 == 0 else 1))
    offset = first_channel // step
    in_specs = [pl.BlockSpec((step, depth, two_rows), lambda c: (c, 0, 0))] * 2 + [
        pl.BlockSpec((step, depth, cols), lambda c: (c, 0, 0))
    ] * 2
    args = [lhs[0], lhs[1], rhs[0], rhs[1]]
    aliases = {}
    if prev is not None:
        in_specs.append(pl.BlockSpec(memory_space=pl.ANY))
        args.append(prev)
        aliases = {4: 0}
    flops = 4 * count * two_rows * depth * cols
    out_bytes = count * two_rows * cols * 4
    return pl.pallas_call(
        functools.partial(correlate_kernel, 1.0 / depth),
        grid=(count // step,),
        in_specs=in_specs,
        out_specs=pl.BlockSpec((step, 2, rows, cols), lambda c: (c + offset, 0, 0, 0)),
        out_shape=jax.ShapeDtypeStruct((own_channels, 2, rows, cols), jnp.float32),
        input_output_aliases=aliases,
        cost_estimate=pl.CostEstimate(
            flops=flops, bytes_accessed=out_bytes + 2 * (lhs[0].size + rhs[0].size) * 2, transcendentals=0
        ),
    )(*args)


def send_chunk(blocks, inp_at, tm_at, inp_size, tm_size):
    group_size = blocks.shape[0]
    pieces = []
    for inp_step in range(inp_size):
        for tm_step in range(tm_size):
            target = ((inp_at + inp_step) % inp_size) * tm_size + (tm_at + tm_step) % tm_size
            block = lax.dynamic_index_in_dim(blocks, target, 0, keepdims=False)
            if inp_step or tm_step:
                route = [
                    (g, ((g // tm_size + inp_step) % inp_size) * tm_size + (g % tm_size + tm_step) % tm_size)
                    for g in range(group_size)
                ]
                block = lax.ppermute(block, ("inp", "tm"), route)
            pieces.append(block)
    return pieces


def assemble_chunk(pieces, inp_at, inp_size, tm_size, cols):
    own_channels, _, spectra_here, inputs_here = pieces[0].shape
    half = jnp.zeros((own_channels, 2, tm_size, spectra_here, cols), jnp.bfloat16)
    for inp_step in range(inp_size):
        for tm_step in range(tm_size):
            block = pieces[inp_step * tm_size + tm_step]
            source_inp = (inp_at + inp_size - inp_step) % inp_size
            half = lax.dynamic_update_slice(
                half, block[:, :, None], (0, 0, tm_step, 0, source_inp * inputs_here)
            )
    return half


def finish_chunk(half, pol_size, cols):
    own_channels, _, tm_size, spectra_here, _ = half.shape
    if pol_size != 2:
        raise ValueError("pol size")
    partner = lax.ppermute(half, "pol", [(0, 1), (1, 0)])
    depth = 2 * tm_size * spectra_here
    rows_here = cols // pol_size
    row_start = lax.axis_index("pol") * rows_here
    lhs, rhs = [], []
    for part in (half, partner):
        own_rows = lax.dynamic_slice_in_dim(part, row_start, rows_here, 4)
        swapped = jnp.stack([own_rows[:, 1], -own_rows[:, 0]], axis=1)
        lhs.append(jnp.concatenate([own_rows, swapped], axis=4).reshape(own_channels, depth, 2 * rows_here))
        rhs.append(part.reshape(own_channels, depth, cols))
    return lhs, rhs


def solution(mesh):
    return jax.shard_map(
        per_device,
        mesh=mesh,
        in_specs=(P(("group", "inp"), ("tm", "pol")),),
        out_specs=P(("group", "inp", "tm"), None, "pol", None),
        check_vma=False,
    )
```
